128 devices in a mesh: section: 4 (over x), dp: 32 (over y, z, core).
Axes of the slice: x: 4, y: 4, z: 4, core: 2. Of those that a mesh axis runs over, the one named last changes fastest.
Arguments:
- section_inputs: bfloat16 [4, 4, 64, 8, 8, 512], P('section', None, 'dp'), may hold values from -6 to 6
- grad_out: bfloat16 [4, 64, 8, 8, 512], P(None, 'dp'), may hold values from -6 to 6
- point_weights: bfloat16 [4, 4, 512, 512], P('section'), may hold values from -0.125 to 0.125
- depth_weights: bfloat16 [4, 4, 9, 512], P('section'), may hold values from -2 to 2
Outputs:
- grad_inputs: bfloat16 [4, 4, 64, 8, 8, 512], P('section', None, 'dp')
- grad_point: float32 [4, 4, 512, 512], P('section', None, 'dp')
- grad_depth: float32 [4, 4, 9, 512], P('section', None, None, 'dp')
The draws below stay inside these ranges and needn't reach their ends.
All inputs are finite; a program needn't handle non-finite values.
Results may differ from the reference program's by a relative error of at most 0.022.
Values may be sent and summed in bfloat16 or wider, within the bound.
No kernel may reach another device: no remote copies, remote signals or barrier semaphores. Data moves between devices by JAX's collectives and lax.ppermute only.
A program may use at most 128 MiB of HBM per device.

```python
import jax
import jax.numpy as jnp
from jax import lax

C = 512
LAYERS = 4
MB = 4
IMG = 8
SECTIONS = 4
BATCH = 64


def steps_of(key, extent, pieces, low, high):
    level, own = 1.0, jax.random.fold_in(key, 6)
    for position, shards_of in pieces:
        steps = jnp.exp(jax.random.uniform(jax.random.fold_in(own, position), (shards_of,), jnp.float32, low / len(pieces), high / len(pieces)))
        level = level * jnp.repeat(steps, extent[position] // shards_of).reshape([-1 if axis == position else 1 for axis in range(len(extent))])
    return level


def bell_draw(own_key, shape, deviation, most, shards=(), kind=jnp.bfloat16):
    values = deviation * jax.random.normal(own_key, shape, jnp.float32)
    if shards:
        values = values * steps_of(own_key, shape, shards, -0.22, 0.18)
    return jnp.clip(values, -most, most).astype(kind)


def setup_inputs(seed: int = 0) -> dict:
    seeds = jax.random.split(jax.random.key(seed), 5)
    return {
        "section_inputs": bell_draw(seeds[0], (SECTIONS, MB, BATCH, IMG, IMG, C), 1.0, 6.0, ((0, 4), (2, 32))),
        "grad_out": bell_draw(seeds[1], (MB, BATCH, IMG, IMG, C), 1.0, 6.0, ((1, 32),)),
        "point_weights": bell_draw(seeds[2], (SECTIONS, LAYERS, C, C), (4 * C) ** -0.5, 0.125, ((0, 4),)),
        "depth_weights": bell_draw(seeds[3], (SECTIONS, LAYERS, 9, C), 9 ** -0.5, 2.0, ((0, 4),)),
    }


def depthwise(field, kern):
    padded = jnp.pad(field, ((0, 0), (1, 1), (1, 1), (0, 0)))
    size = field.shape[1]
    total = jnp.zeros(field.shape, jnp.float32)
    for di in range(3):
        for dj in range(3):
            total = total + kern[3 * di + dj] * padded[:, di:di + size, dj:dj + size, :]
    return total

def depthwise_back(grad, kern):
    padded = jnp.pad(grad, ((0, 0), (1, 1), (1, 1), (0, 0)))
    size = grad.shape[1]
    total = jnp.zeros(grad.shape, jnp.float32)
    for di in range(3):
        for dj in range(3):
            total = total + kern[3 * di + dj] * padded[:, 2 - di:2 - di + size, 2 - dj:2 - dj + size, :]
    return total

def kernel_grad(field, grad):
    padded = jnp.pad(field, ((0, 0), (1, 1), (1, 1), (0, 0)))
    size = field.shape[1]
    taps = []
    for di in range(3):
        for dj in range(3):
            taps.append(lax.optimization_barrier(jnp.sum(padded[:, di:di + size, dj:dj + size, :] * grad, axis=(0, 1, 2))))
    return jnp.stack(taps)

def section_backward(field, grad, weights, kerns):
    chans = field.shape[-1]
    inputs, zeds, acts = ([], [], [])
    for layer in range(weights.shape[0]):
        kern = kerns[layer].astype(jnp.float32)
        zed = depthwise(field.astype(jnp.float32), kern)
        act = jax.nn.silu(zed).astype(jnp.bfloat16)
        branch = jnp.dot(act.reshape(-1, chans), weights[layer], preferred_element_type=jnp.float32)
        inputs.append(field)
        zeds.append(zed)
        acts.append(act)
        field = (field.astype(jnp.float32) + branch.reshape(field.shape)).astype(jnp.bfloat16)
    point_list, depth_list = ([], [])
    for layer in reversed(range(weights.shape[0])):
        flat = grad.reshape(-1, chans)
        point_list.append(jnp.dot(acts[layer].reshape(-1, chans).T, flat, preferred_element_type=jnp.float32))
        back = jnp.dot(flat, weights[layer].T, preferred_element_type=jnp.float32).reshape(grad.shape)
        sig = jax.nn.sigmoid(zeds[layer])
        dzed = back * sig * (1.0 + zeds[layer] * (1.0 - sig))
        depth_list.append(kernel_grad(inputs[layer].astype(jnp.float32), dzed))
        kern = kerns[layer].astype(jnp.float32)
        grad = (grad.astype(jnp.float32) + depthwise_back(dzed, kern)).astype(jnp.bfloat16)
    return (grad, jnp.stack(point_list[::-1]), jnp.stack(depth_list[::-1]))

def reference(section_inputs, grad_out, point_weights, depth_weights):
    shape = grad_out.shape
    flat_shape = (shape[0] * shape[1], shape[2], shape[3], shape[4])
    grad = grad_out.reshape(flat_shape)
    grads, points, depths = ([None] * SECTIONS, [None] * SECTIONS, [None] * SECTIONS)
    for section in reversed(range(SECTIONS)):
        field = section_inputs[section].reshape(flat_shape)
        grad, gpoint, gdepth = section_backward(field, grad, point_weights[section], depth_weights[section])
        grads[section] = grad.reshape(shape)
        points[section] = gpoint
        depths[section] = gdepth
    scale = jnp.float32(1.0) / jnp.sqrt(jnp.float32(shape[0] * shape[1] * shape[2] * shape[3]))
    return (jnp.stack(grads), jnp.stack(points) * scale, jnp.stack(depths) * scale)
```

```python
import jax
import jax.numpy as jnp
from jax import lax
from jax.sharding import PartitionSpec as P


def from_behind(shard, axis, by):
    devices = lax.axis_size(axis)
    pairs = [(i, i + by) for i in range(devices) if 0 <= i + by < devices]
    return lax.ppermute(shard, axis, pairs)


def depthwise(field, kern):
    padded = jnp.pad(field, ((0, 0), (1, 1), (1, 1), (0, 0)))
    size = field.shape[1]
    total = jnp.zeros(field.shape, jnp.float32)
    for di in range(3):
        for dj in range(3):
            total = total + kern[3 * di + dj] * padded[:, di : di + size, dj : dj + size, :]
    return total


def depthwise_back(grad, kern):
    padded = jnp.pad(grad, ((0, 0), (1, 1), (1, 1), (0, 0)))
    size = grad.shape[1]
    total = jnp.zeros(grad.shape, jnp.float32)
    for di in range(3):
        for dj in range(3):
            total = (
                total
                + kern[3 * di + dj] * padded[:, 2 - di : 2 - di + size, 2 - dj : 2 - dj + size, :]
            )
    return total


def kernel_grad(field, grad):
    padded = jnp.pad(field, ((0, 0), (1, 1), (1, 1), (0, 0)))
    size = field.shape[1]
    taps = []
    for di in range(3):
        for dj in range(3):
            taps.append(
                jnp.sum(padded[:, di : di + size, dj : dj + size, :] * grad, axis=(0, 1, 2))
            )
    return jnp.stack(taps)


def body(section_inputs, grad_out, point_weights, depth_weights):
    sections = lax.axis_size("section")
    replicas = lax.axis_size("dp")
    my_section = lax.axis_index("section")
    batches = grad_out.shape[0]
    layers = point_weights.shape[1]
    chans = point_weights.shape[3]
    taps = depth_weights.shape[2]
    inputs = section_inputs[0]
    weights = point_weights[0]
    kerns = depth_weights[0].astype(jnp.float32)
    mb_shape = inputs.shape[1:]

    field = inputs.reshape((-1,) + inputs.shape[2:])
    saved_in, saved_z, saved_a = ([], [], [])
    for layer in range(layers):
        zed = depthwise(field.astype(jnp.float32), kerns[layer])
        act = jax.nn.silu(zed).astype(jnp.bfloat16)
        branch = jnp.dot(
            act.reshape(-1, chans), weights[layer], preferred_element_type=jnp.float32
        )
        saved_in.append(field)
        saved_z.append(zed.reshape((batches,) + mb_shape))
        saved_a.append(act)
        field = (field.astype(jnp.float32) + branch.reshape(field.shape)).astype(jnp.bfloat16)

    total_steps = batches + sections - 1
    g_slots = [[] for layer in range(layers)]
    dz_slots = [[] for layer in range(layers)]
    out_slots = []
    carried = jnp.zeros(mb_shape, jnp.bfloat16)
    for step in range(total_steps):
        batch_id = step - (sections - 1) + my_section
        valid = (batch_id >= 0) & (batch_id < batches)
        picked = jnp.clip(batch_id, 0, batches - 1)
        top = lax.dynamic_index_in_dim(grad_out, picked, 0, keepdims=False)
        grad = jnp.where(my_section == sections - 1, top, carried)
        grad = jnp.where(valid, grad, jnp.zeros_like(grad))
        for layer in reversed(range(layers)):
            zed = lax.dynamic_index_in_dim(saved_z[layer], picked, 0, keepdims=False)
            g_slots[layer].append(grad)
            flat = grad.reshape(-1, chans)
            back = jnp.dot(flat, weights[layer].T, preferred_element_type=jnp.float32).reshape(
                grad.shape
            )
            sig = jax.nn.sigmoid(zed)
            dzed = back * sig * (1.0 + zed * (1.0 - sig))
            dz_slots[layer].append(dzed)
            grad = (grad.astype(jnp.float32) + depthwise_back(dzed, kerns[layer])).astype(
                jnp.bfloat16
            )
        out_slots.append(grad)
        if step < total_steps - 1:
            carried = from_behind(grad, "section", -1)

    first = sections - 1 - my_section
    results = lax.dynamic_slice_in_dim(jnp.stack(out_slots), first, batches, 0)

    point_list, depth_list = ([], [])
    for layer in range(layers):
        g_all = lax.dynamic_slice_in_dim(jnp.stack(g_slots[layer]), first, batches, 0)
        dz_all = lax.dynamic_slice_in_dim(jnp.stack(dz_slots[layer]), first, batches, 0)
        point_list.append(
            jnp.dot(
                saved_a[layer].reshape(-1, chans).T,
                g_all.reshape(-1, chans),
                preferred_element_type=jnp.float32,
            )
        )
        depth_list.append(
            kernel_grad(
                saved_in[layer].astype(jnp.float32), dz_all.reshape((-1,) + mb_shape[1:])
            )
        )

    count = batches * inputs.shape[1] * replicas * inputs.shape[2] * inputs.shape[3]
    scale = jnp.float32(1.0) / jnp.sqrt(jnp.float32(count))
    share = chans // replicas
    point = jnp.stack(point_list) * scale
    depth = jnp.stack(depth_list) * scale
    send_point = point.reshape(layers, replicas, share * chans).transpose(1, 0, 2)
    send_point = send_point.reshape(replicas, layers * share * chans)
    send_depth = depth.reshape(layers, taps, replicas, share).transpose(2, 0, 1, 3)
    send_depth = send_depth.reshape(replicas, layers * taps * share)
    depth_len = layers * taps * share
    pad = (-depth_len) % 128
    send = jnp.concatenate(
        [send_point, send_depth, jnp.zeros((replicas, pad), jnp.float32)], axis=1
    ).astype(jnp.bfloat16)
    recv = lax.all_to_all(send, "dp", 0, 0, tiled=True)
    summed = jnp.sum(recv.astype(jnp.float32), axis=0)
    point_len = layers * share * chans
    point_red = summed[:point_len].reshape(layers, share, chans)
    depth_red = summed[point_len : point_len + depth_len].reshape(layers, taps, share)
    return (results[None], point_red[None], depth_red[None])


def solution(mesh):
    return jax.shard_map(
        body,
        mesh=mesh,
        in_specs=(
            P("section", None, "dp", None, None, None),
            P(None, "dp", None, None, None),
            P("section", None, None, None),
            P("section", None, None, None),
        ),
        out_specs=(
            P("section", None, "dp", None, None, None),
            P("section", None, "dp", None),
            P("section", None, None, "dp"),
        ),
        check_vma=False,
    )
```

```python
import functools

import jax
import jax.numpy as jnp
from jax import lax
from jax.experimental import pallas as pl
from jax.experimental.pallas import tpu as pltpu
from jax.sharding import PartitionSpec as P

VMEM_LIMIT = 60 * 1024 * 1024


def from_behind(shard, axis, by):
    devices = lax.axis_size(axis)
    pairs = [(i, i + by) for i in range(devices) if 0 <= i + by < devices]
    return lax.ppermute(shard, axis, pairs)


def shift_rows(x, off):
    rows = x.shape[0]
    amount = (-off) % rows
    return x if amount == 0 else pltpu.roll(x, amount, 0)


def tap_mask(shape, di, dj, height, width):
    r = lax.broadcasted_iota(jnp.int32, shape, 0)
    j = lax.rem(r, width)
    i = lax.rem(lax.div(r, width), height)
    return (i + di >= 0) & (i + di < height) & (j + dj >= 0) & (j + dj < width)


def offsets():
    for di in (-1, 0, 1):
        for dj in (-1, 0, 1):
            yield 3 * (di + 1) + (dj + 1), di, dj


def stencil(x, k_ref, layer, height, width, sign):
    total = jnp.zeros(x.shape, jnp.float32)
    for tap, di, dj in offsets():
        di_s, dj_s = sign * di, sign * dj
        moved = shift_rows(x, di_s * width + dj_s)
        moved = jnp.where(tap_mask(x.shape, di_s, dj_s, height, width), moved, 0.0)
        total = total + k_ref[layer, tap : tap + 1, :] * moved
    return total


def fwd_kernel(x_ref, w_ref, k_ref, z_ref, a_ref, xs_ref, *, height, width):
    layers = w_ref.shape[0]
    field = x_ref[...]
    for layer in range(layers):
        xs_ref[layer] = field
        xf = field.astype(jnp.float32)
        zed = stencil(xf, k_ref, layer, height, width, 1)
        z_ref[layer] = zed
        act = (zed * jax.nn.sigmoid(zed)).astype(jnp.bfloat16)
        a_ref[layer] = act
        branch = jnp.dot(act, w_ref[layer], preferred_element_type=jnp.float32)
        field = (xf + branch).astype(jnp.bfloat16)


def step_kernel(p_ref, top_ref, car_ref, z_ref, w_ref, k_ref, h_in, g_ref, h_ref, *, height, width):
    del h_in
    layers = w_ref.shape[0]
    top = top_ref[...].astype(jnp.float32)
    car = car_ref[...].astype(jnp.float32)
    g = jnp.where(p_ref[1] == 1, top, car)
    g = jnp.where(p_ref[2] == 1, g, 0.0).astype(jnp.bfloat16)
    h_ref[layers] = g
    for layer in reversed(range(layers)):
        back = lax.dot_general(
            g, w_ref[layer], (((1,), (1,)), ((), ())), preferred_element_type=jnp.float32
        )
        zed = z_ref[layer]
        sig = jax.nn.sigmoid(zed)
        dzed = back * sig * (1.0 + zed * (1.0 - sig))
        g = (g.astype(jnp.float32) + stencil(dzed, k_ref, layer, height, width, -1)).astype(
            jnp.bfloat16
        )
        h_ref[layer] = g
    g_ref[...] = g


def grad_kernel(
    p_ref, h_ref, a_ref, xs_ref, z_ref, w_ref, k_ref, send_ref, res_ref, *, height, width, scale
):
    layers, chans = w_ref.shape[0], w_ref.shape[2]
    taps = k_ref.shape[1]
    batches = res_ref.shape[0]
    rows = h_ref.shape[2]
    replicas = send_ref.shape[0]
    share = chans // replicas
    pad_taps = send_ref.shape[1] - layers * share
    first = p_ref[0]
    for m in range(batches):
        res_ref[m] = h_ref[0, first + m]
    depth = []
    for layer in range(layers):
        g = h_ref[layer + 1, pl.ds(first, batches)].reshape(batches * rows, chans)
        back = lax.dot_general(
            g, w_ref[layer], (((1,), (1,)), ((), ())), preferred_element_type=jnp.float32
        )
        zed = z_ref[layer]
        sig = jax.nn.sigmoid(zed)
        dzed = back * sig * (1.0 + zed * (1.0 - sig))
        point = lax.dot_general(
            a_ref[layer], g, (((0,), (0,)), ((), ())), preferred_element_type=jnp.float32
        )
        point = point * scale
        for d in range(replicas):
            send_ref[d, layer * share : (layer + 1) * share, :] = point[
                d * share : (d + 1) * share
            ].astype(jnp.bfloat16)
        xf = xs_ref[layer].astype(jnp.float32)
        rows_out = []
        for tap, di, dj in offsets():
            moved = shift_rows(xf, di * width + dj)
            moved = jnp.where(tap_mask(xf.shape, di, dj, height, width), moved, 0.0)
            rows_out.append(jnp.sum(moved * dzed, axis=0, keepdims=True))
        rows_out.append(jnp.zeros((pad_taps - taps, chans), jnp.float32))
        depth.append(jnp.concatenate(rows_out, axis=0) * scale)
    lane = lax.broadcasted_iota(jnp.int32, (pad_taps, chans), 1)
    for d in range(replicas):
        slot = jnp.zeros((pad_taps, chans), jnp.float32)
        for layer in range(layers):
            amount = (layer * share - d * share) % chans
            moved = depth[layer] if amount == 0 else pltpu.roll(depth[layer], amount, 1)
            keep = (lane >= layer * share) & (lane < (layer + 1) * share)
            slot = jnp.where(keep, moved, slot)
        send_ref[d, layers * share :, :] = slot.astype(jnp.bfloat16)


def body(section_inputs, grad_out, point_weights, depth_weights):
    sections = lax.axis_size("section")
    replicas = lax.axis_size("dp")
    my_section = lax.axis_index("section")
    batches = grad_out.shape[0]
    layers = point_weights.shape[1]
    chans = point_weights.shape[3]
    taps = depth_weights.shape[2]
    inputs = section_inputs[0]
    images, height, width = inputs.shape[1], inputs.shape[2], inputs.shape[3]
    rows = images * height * width
    weights = point_weights[0]
    kerns = depth_weights[0].astype(jnp.float32)
    vmem = pl.BlockSpec(memory_space=pltpu.VMEM)
    smem = pl.BlockSpec(memory_space=pltpu.SMEM)
    params = pltpu.CompilerParams(vmem_limit_bytes=VMEM_LIMIT)

    zs, acts, xs = pl.pallas_call(
        functools.partial(fwd_kernel, height=height, width=width),
        out_shape=(
            jax.ShapeDtypeStruct((layers, batches * rows, chans), jnp.float32),
            jax.ShapeDtypeStruct((layers, batches * rows, chans), jnp.bfloat16),
            jax.ShapeDtypeStruct((layers, batches * rows, chans), jnp.bfloat16),
        ),
        in_specs=[vmem, vmem, vmem],
        out_specs=(vmem, vmem, vmem),
        compiler_params=params,
    )(inputs.reshape(batches * rows, chans), weights, kerns)
    z_mb = zs.reshape(layers, batches, rows, chans)
    top_all = grad_out.reshape(batches, rows, chans)

    total_steps = batches + sections - 1
    hbuf = jnp.zeros((layers + 1, total_steps, rows, chans), jnp.bfloat16)
    carried = jnp.zeros((rows, chans), jnp.bfloat16)
    is_last = (my_section == sections - 1).astype(jnp.int32)
    for step in range(total_steps):
        batch_id = step - (sections - 1) + my_section
        valid = ((batch_id >= 0) & (batch_id < batches)).astype(jnp.int32)
        picked = jnp.clip(batch_id, 0, batches - 1)
        scalars = jnp.stack([picked, is_last, valid]).astype(jnp.int32)
        grid_spec = pltpu.PrefetchScalarGridSpec(
            num_scalar_prefetch=1,
            grid=(1,),
            in_specs=[
                pl.BlockSpec((None, rows, chans), lambda i, p: (p[0], 0, 0)),
                pl.BlockSpec((rows, chans), lambda i, p: (0, 0)),
                pl.BlockSpec((layers, None, rows, chans), lambda i, p: (0, p[0], 0, 0)),
                pl.BlockSpec((layers, chans, chans), lambda i, p: (0, 0, 0)),
                pl.BlockSpec((layers, taps, chans), lambda i, p: (0, 0, 0)),
                pl.BlockSpec(memory_space=pl.ANY),
            ],
            out_specs=[
                pl.BlockSpec((rows, chans), lambda i, p: (0, 0)),
                pl.BlockSpec(
                    (layers + 1, None, rows, chans), lambda i, p, s=step: (0, s, 0, 0)
                ),
            ],
        )
        g, hbuf = pl.pallas_call(
            functools.partial(step_kernel, height=height, width=width),
            out_shape=(
                jax.ShapeDtypeStruct((rows, chans), jnp.bfloat16),
                jax.ShapeDtypeStruct(hbuf.shape, jnp.bfloat16),
            ),
            grid_spec=grid_spec,
            input_output_aliases={6: 1},
            compiler_params=params,
        )(scalars, top_all, carried, z_mb, weights, kerns, hbuf)
        if step < total_steps - 1:
            carried = from_behind(g, "section", -1)

    count = batches * images * replicas * height * width
    scale = 1.0 / float(count) ** 0.5
    share = chans // replicas
    pad_taps = -(-taps // 16) * 16
    first = jnp.reshape(sections - 1 - my_section, (1,)).astype(jnp.int32)
    send, res = pl.pallas_call(
        functools.partial(grad_kernel, height=height, width=width, scale=scale),
        out_shape=(
            jax.ShapeDtypeStruct((replicas, layers * share + pad_taps, chans), jnp.bfloat16),
            jax.ShapeDtypeStruct((batches, rows, chans), jnp.bfloat16),
        ),
        in_specs=[smem, vmem, vmem, vmem, vmem, vmem, vmem],
        out_specs=(vmem, vmem),
        compiler_params=params,
    )(first, hbuf, acts, xs, zs, weights, kerns)
    recv = lax.all_to_all(send, "dp", 0, 0, tiled=True)
    summed = jnp.sum(recv.astype(jnp.float32), axis=0)
    point_red = summed[: layers * share].reshape(layers, share, chans)
    depth_red = summed[layers * share : layers * share + taps, : layers * share]
    depth_red = depth_red.reshape(taps, layers, share).transpose(1, 0, 2)
    results = res.reshape(inputs.shape)
    return (results[None], point_red[None], depth_red[None])


def solution(mesh):
    return jax.shard_map(
        body,
        mesh=mesh,
        in_specs=(
            P("section", None, "dp", None, None, None),
            P(None, "dp", None, None, None),
            P("section", None, None, None),
            P("section", None, None, None),
        ),
        out_specs=(
            P("section", None, "dp", None, None, None),
            P("section", None, "dp", None),
            P("section", None, None, "dp"),
        ),
        check_vma=False,
    )
```

```python
import functools

import jax
import jax.numpy as jnp
from jax import lax
from jax.experimental import pallas as pl
from jax.experimental.pallas import tpu as pltpu
from jax.sharding import PartitionSpec as P

VMEM_LIMIT = 60 * 1024 * 1024


def from_behind(shard, axis, by):
    devices = lax.axis_size(axis)
    pairs = [(i, i + by) for i in range(devices) if 0 <= i + by < devices]
    return lax.ppermute(shard, axis, pairs)


def shift_rows(x, off):
    rows = x.shape[0]
    amount = (-off) % rows
    return x if amount == 0 else pltpu.roll(x, amount, 0)


def tap_mask(shape, di, dj, height, width):
    r = lax.broadcasted_iota(jnp.int32, shape, 0)
    j = lax.rem(r, width)
    i = lax.rem(lax.div(r, width), height)
    return (i + di >= 0) & (i + di < height) & (j + dj >= 0) & (j + dj < width)


def offsets():
    for di in (-1, 0, 1):
        for dj in (-1, 0, 1):
            yield 3 * (di + 1) + (dj + 1), di, dj


def stencil(x, k_ref, layer, height, width, sign):
    total = jnp.zeros(x.shape, jnp.float32)
    for tap, di, dj in offsets():
        di_s, dj_s = sign * di, sign * dj
        moved = shift_rows(x, di_s * width + dj_s)
        moved = jnp.where(tap_mask(x.shape, di_s, dj_s, height, width), moved, 0.0)
        total = total + k_ref[layer, tap : tap + 1, :] * moved
    return total


def fwd_kernel(p_ref, x_ref, w_ref, k_ref, *refs, height, width):
    z_ref, a_ref, xs_ref = refs[-3:]
    layers = w_ref.shape[0]
    field = x_ref[...]
    for layer in range(layers):
        xs_ref[layer] = field
        xf = field.astype(jnp.float32)
        zed = stencil(xf, k_ref, layer, height, width, 1)
        z_ref[layer] = zed
        act = (zed * jax.nn.sigmoid(zed)).astype(jnp.bfloat16)
        a_ref[layer] = act
        branch = jnp.dot(act, w_ref[layer], preferred_element_type=jnp.float32)
        field = (xf + branch).astype(jnp.bfloat16)


def fwd_first_kernel(p_ref, x_ref, w_ref, k_ref, z_ref, a_ref, xs_ref, h_ref, *, height, width):
    del h_ref
    fwd_kernel(p_ref, x_ref, w_ref, k_ref, z_ref, a_ref, xs_ref, height=height, width=width)


def step_kernel(p_ref, top_ref, car_ref, z_ref, w_ref, k_ref, h_in, g_ref, h_ref, *, height, width):
    del h_in
    layers = w_ref.shape[0]
    top = top_ref[...].astype(jnp.float32)
    car = car_ref[...].astype(jnp.float32)
    g = jnp.where(p_ref[1] == 1, top, car)
    g = jnp.where(p_ref[2] == 1, g, 0.0).astype(jnp.bfloat16)
    h_ref[layers] = g
    for layer in reversed(range(layers)):
        back = lax.dot_general(
            g, w_ref[layer], (((1,), (1,)), ((), ())), preferred_element_type=jnp.float32
        )
        zed = z_ref[layer]
        sig = jax.nn.sigmoid(zed)
        dzed = back * sig * (1.0 + zed * (1.0 - sig))
        g = (g.astype(jnp.float32) + stencil(dzed, k_ref, layer, height, width, -1)).astype(
            jnp.bfloat16
        )
        h_ref[layer] = g
    g_ref[...] = g


def grad_kernel(
    p_ref, h_ref, a_ref, xs_ref, z_ref, w_ref, k_ref, send_ref, res_ref, *, height, width, scale
):
    layers, chans = w_ref.shape[0], w_ref.shape[2]
    taps = k_ref.shape[1]
    batches = res_ref.shape[0]
    rows = h_ref.shape[2]
    replicas = send_ref.shape[0]
    share = chans // replicas
    pad_taps = send_ref.shape[1] - layers * share
    first = p_ref[0]
    for m in range(batches):
        res_ref[m] = h_ref[0, first + m]
    depth = []
    for layer in range(layers):
        g = h_ref[layer + 1, pl.ds(first, batches)].reshape(batches * rows, chans)
        back = lax.dot_general(
            g, w_ref[layer], (((1,), (1,)), ((), ())), preferred_element_type=jnp.float32
        )
        zed = z_ref[layer]
        sig = jax.nn.sigmoid(zed)
        dzed = back * sig * (1.0 + zed * (1.0 - sig))
        point = lax.dot_general(
            a_ref[layer], g, (((0,), (0,)), ((), ())), preferred_element_type=jnp.float32
        )
        point = point * scale
        for d in range(replicas):
            send_ref[d, layer * share : (layer + 1) * share, :] = point[
                d * share : (d + 1) * share
            ].astype(jnp.bfloat16)
        xf = xs_ref[layer].astype(jnp.float32)
        rows_out = []
        for tap, di, dj in offsets():
            moved = shift_rows(xf, di * width + dj)
            moved = jnp.where(tap_mask(xf.shape, di, dj, height, width), moved, 0.0)
            rows_out.append(jnp.sum(moved * dzed, axis=0, keepdims=True))
        rows_out.append(jnp.zeros((pad_taps - taps, chans), jnp.float32))
        depth.append(jnp.concatenate(rows_out, axis=0) * scale)
    lane = lax.broadcasted_iota(jnp.int32, (pad_taps, chans), 1)
    for d in range(replicas):
        slot = jnp.zeros((pad_taps, chans), jnp.float32)
        for layer in range(layers):
            amount = (layer * share - d * share) % chans
            moved = depth[layer] if amount == 0 else pltpu.roll(depth[layer], amount, 1)
            keep = (lane >= layer * share) & (lane < (layer + 1) * share)
            slot = jnp.where(keep, moved, slot)
        send_ref[d, layers * share :, :] = slot.astype(jnp.bfloat16)


def body(section_inputs, grad_out, point_weights, depth_weights):
    sections = lax.axis_size("section")
    replicas = lax.axis_size("dp")
    my_section = lax.axis_index("section")
    batches = grad_out.shape[0]
    layers = point_weights.shape[1]
    chans = point_weights.shape[3]
    taps = depth_weights.shape[2]
    inputs = section_inputs[0]
    images, height, width = inputs.shape[1], inputs.shape[2], inputs.shape[3]
    rows = images * height * width
    weights = point_weights[0]
    kerns = depth_weights[0].astype(jnp.float32)
    vmem = pl.BlockSpec(memory_space=pltpu.VMEM)
    smem = pl.BlockSpec(memory_space=pltpu.SMEM)
    params = pltpu.CompilerParams(vmem_limit_bytes=VMEM_LIMIT)

    fwd_flops = 2 * layers * rows * chans * (chans + 3 * taps)
    fwd_cost = pl.CostEstimate(
        flops=fwd_flops,
        transcendentals=layers * rows * chans,
        bytes_accessed=2 * layers * chans * chans + 8 * layers * rows * chans,
    )
    top_all = grad_out.reshape(batches, rows, chans)
    x_all = inputs.reshape(batches, rows, chans)
    total_steps = batches + sections - 1
    buf_shapes = (
        jax.ShapeDtypeStruct((layers, batches, rows, chans), jnp.float32),
        jax.ShapeDtypeStruct((layers, batches, rows, chans), jnp.bfloat16),
        jax.ShapeDtypeStruct((layers, batches, rows, chans), jnp.bfloat16),
    )
    slot_spec = pl.BlockSpec((layers, None, rows, chans), lambda i, p: (0, p[0], 0, 0))
    fwd_in = [
        pl.BlockSpec((None, rows, chans), lambda i, p: (p[0], 0, 0)),
        pl.BlockSpec((layers, chans, chans), lambda i, p: (0, 0, 0)),
        pl.BlockSpec((layers, taps, chans), lambda i, p: (0, 0, 0)),
    ]

    def picked_at(step):
        batch_id = step - (sections - 1) + my_section
        valid = ((batch_id >= 0) & (batch_id < batches)).astype(jnp.int32)
        return jnp.clip(batch_id, 0, batches - 1), valid

    picked, _ = picked_at(0)
    zbuf, abuf, xbuf, hbuf = pl.pallas_call(
        functools.partial(fwd_first_kernel, height=height, width=width),
        out_shape=buf_shapes
        + (jax.ShapeDtypeStruct((layers + 1, total_steps, rows, chans), jnp.bfloat16),),
        grid_spec=pltpu.PrefetchScalarGridSpec(
            num_scalar_prefetch=1,
            grid=(1,),
            in_specs=fwd_in,
            out_specs=[slot_spec, slot_spec, slot_spec, pl.BlockSpec(memory_space=pl.ANY)],
        ),
        compiler_params=params,
        cost_estimate=fwd_cost,
    )(jnp.reshape(picked, (1,)).astype(jnp.int32), x_all, weights, kerns)

    carried = jnp.zeros((rows, chans), jnp.bfloat16)
    is_last = (my_section == sections - 1).astype(jnp.int32)
    for step in range(total_steps):
        picked, valid = picked_at(step)
        scalars = jnp.stack([picked, is_last, valid]).astype(jnp.int32)
        grid_spec = pltpu.PrefetchScalarGridSpec(
            num_scalar_prefetch=1,
            grid=(1,),
            in_specs=[
                pl.BlockSpec((None, rows, chans), lambda i, p: (p[0], 0, 0)),
                pl.BlockSpec((rows, chans), lambda i, p: (0, 0)),
                pl.BlockSpec((layers, None, rows, chans), lambda i, p: (0, p[0], 0, 0)),
                pl.BlockSpec((layers, chans, chans), lambda i, p: (0, 0, 0)),
                pl.BlockSpec((layers, taps, chans), lambda i, p: (0, 0, 0)),
                pl.BlockSpec(memory_space=pl.ANY),
            ],
            out_specs=[
                pl.BlockSpec((rows, chans), lambda i, p: (0, 0)),
                pl.BlockSpec(
                    (layers + 1, None, rows, chans), lambda i, p, s=step: (0, s, 0, 0)
                ),
            ],
        )
        g, hbuf = pl.pallas_call(
            functools.partial(step_kernel, height=height, width=width),
            out_shape=(
                jax.ShapeDtypeStruct((rows, chans), jnp.bfloat16),
                jax.ShapeDtypeStruct(hbuf.shape, jnp.bfloat16),
            ),
            grid_spec=grid_spec,
            input_output_aliases={6: 1},
            compiler_params=params,
            cost_estimate=fwd_cost,
        )(scalars, top_all, carried, zbuf, weights, kerns, hbuf)
        if step < total_steps - 1:
            carried = from_behind(g, "section", -1)
            nxt, _ = picked_at(step + 1)
            zbuf, abuf, xbuf = pl.pallas_call(
                functools.partial(fwd_kernel, height=height, width=width),
                out_shape=buf_shapes,
                grid_spec=pltpu.PrefetchScalarGridSpec(
                    num_scalar_prefetch=1,
                    grid=(1,),
                    in_specs=fwd_in + [pl.BlockSpec(memory_space=pl.ANY)] * 3,
                    out_specs=[slot_spec, slot_spec, slot_spec],
                ),
                input_output_aliases={4: 0, 5: 1, 6: 2},
                compiler_params=params,
                cost_estimate=fwd_cost,
            )(jnp.reshape(nxt, (1,)).astype(jnp.int32), x_all, weights, kerns, zbuf, abuf, xbuf)
    zs = zbuf.reshape(layers, batches * rows, chans)
    acts = abuf.reshape(layers, batches * rows, chans)
    xs = xbuf.reshape(layers, batches * rows, chans)

    count = batches * images * replicas * height * width
    scale = 1.0 / float(count) ** 0.5
    share = chans // replicas
    pad_taps = -(-taps // 16) * 16
    first = jnp.reshape(sections - 1 - my_section, (1,)).astype(jnp.int32)
    send, res = pl.pallas_call(
        functools.partial(grad_kernel, height=height, width=width, scale=scale),
        out_shape=(
            jax.ShapeDtypeStruct((replicas, layers * share + pad_taps, chans), jnp.bfloat16),
            jax.ShapeDtypeStruct((batches, rows, chans), jnp.bfloat16),
        ),
        in_specs=[smem, vmem, vmem, vmem, vmem, vmem, vmem],
        out_specs=(vmem, vmem),
        compiler_params=params,
    )(first, hbuf, acts, xs, zs, weights, kerns)
    recv = lax.all_to_all(send, "dp", 0, 0, tiled=True)
    summed = jnp.sum(recv.astype(jnp.float32), axis=0)
    point_red = summed[: layers * share].reshape(layers, share, chans)
    depth_red = summed[layers * share : layers * share + taps, : layers * share]
    depth_red = depth_red.reshape(taps, layers, share).transpose(1, 0, 2)
    results = res.reshape(inputs.shape)
    return (results[None], point_red[None], depth_red[None])


def solution(mesh):
    return jax.shard_map(
        body,
        mesh=mesh,
        in_specs=(
            P("section", None, "dp", None, None, None),
            P(None, "dp", None, None, None),
            P("section", None, None, None),
            P("section", None, None, None),
        ),
        out_specs=(
            P("section", None, "dp", None, None, None),
            P("section", None, "dp", None),
            P("section", None, None, "dp"),
        ),
        check_vma=False,
    )
```

```python
import functools

import jax
import jax.numpy as jnp
from jax import lax
from jax.experimental import pallas as pl
from jax.experimental.pallas import tpu as pltpu
from jax.sharding import PartitionSpec as P

VMEM_LIMIT = 60 * 1024 * 1024


def from_behind(shard, axis, by):
    devices = lax.axis_size(axis)
    pairs = [(i, i + by) for i in range(devices) if 0 <= i + by < devices]
    return lax.ppermute(shard, axis, pairs)


def shift_rows(x, off):
    rows = x.shape[0]
    amount = (-off) % rows
    return x if amount == 0 else pltpu.roll(x, amount, 0)


def edge_masks(shape, height, width):
    r = lax.broadcasted_iota(jnp.int32, shape, 0)
    if width & (width - 1) == 0 and height & (height - 1) == 0:
        j = r & (width - 1)
        i = lax.shift_right_logical(r, width.bit_length() - 1) & (height - 1)
    else:
        j = lax.rem(r, width)
        i = lax.rem(lax.div(r, width), height)
    return {
        ("i", -1): i >= 1,
        ("i", 1): i < height - 1,
        ("j", -1): j >= 1,
        ("j", 1): j < width - 1,
    }


def offsets():
    for di in (-1, 0, 1):
        for dj in (-1, 0, 1):
            yield 3 * (di + 1) + (dj + 1), di, dj


def shifted_taps(x, masks, width, sign):
    cols = {}
    for dj in (-1, 0, 1):
        s = sign * dj
        cols[dj] = x if s == 0 else jnp.where(masks[("j", s)], shift_rows(x, s), 0.0)
    for tap, di, dj in offsets():
        s = sign * di
        c = cols[dj]
        yield tap, (c if s == 0 else jnp.where(masks[("i", s)], shift_rows(c, s * width), 0.0))


def stencil(x, k_ref, layer, masks, width, sign):
    total = jnp.zeros(x.shape, jnp.float32)
    for tap, moved in shifted_taps(x, masks, width, sign):
        total = total + k_ref[layer, tap : tap + 1, :] * moved
    return total


def fwd_kernel(p_ref, x_ref, w_ref, k_ref, *refs, height, width):
    z_ref, a_ref, xs_ref = refs[-3:]
    layers = w_ref.shape[0]
    field = x_ref[...]
    masks = edge_masks(field.shape, height, width)
    for layer in range(layers):
        xs_ref[layer] = field
        xf = field.astype(jnp.float32)
        zed = stencil(xf, k_ref, layer, masks, width, 1)
        z_ref[layer] = zed
        act = (zed * jax.nn.sigmoid(zed)).astype(jnp.bfloat16)
        a_ref[layer] = act
        branch = jnp.dot(act, w_ref[layer], preferred_element_type=jnp.float32)
        field = (xf + branch).astype(jnp.bfloat16)


def fwd_first_kernel(p_ref, x_ref, w_ref, k_ref, z_ref, a_ref, xs_ref, h_ref, *, height, width):
    del h_ref
    fwd_kernel(p_ref, x_ref, w_ref, k_ref, z_ref, a_ref, xs_ref, height=height, width=width)


def step_kernel(p_ref, top_ref, car_ref, z_ref, w_ref, k_ref, h_in, g_ref, h_ref, *, height, width):
    del h_in
    layers = w_ref.shape[0]
    top = top_ref[...].astype(jnp.float32)
    car = car_ref[...].astype(jnp.float32)
    g = jnp.where(p_ref[1] == 1, top, car)
    g = jnp.where(p_ref[2] == 1, g, 0.0).astype(jnp.bfloat16)
    h_ref[layers] = g
    masks = edge_masks(g.shape, height, width)
    for layer in reversed(range(layers)):
        back = lax.dot_general(
            g, w_ref[layer], (((1,), (1,)), ((), ())), preferred_element_type=jnp.float32
        )
        zed = z_ref[layer]
        sig = jax.nn.sigmoid(zed)
        dzed = back * sig * (1.0 + zed * (1.0 - sig))
        g = (g.astype(jnp.float32) + stencil(dzed, k_ref, layer, masks, width, -1)).astype(
            jnp.bfloat16
        )
        h_ref[layer] = g
    g_ref[...] = g


def grad_kernel(
    p_ref, h_ref, a_ref, xs_ref, z_ref, w_ref, k_ref, send_ref, res_ref, *, height, width, scale
):
    layers, chans = w_ref.shape[0], w_ref.shape[2]
    taps = k_ref.shape[1]
    batches = res_ref.shape[0]
    rows = h_ref.shape[2]
    replicas = send_ref.shape[0]
    share = chans // replicas
    pad_taps = send_ref.shape[1] - layers * share
    first = p_ref[0]
    for m in range(batches):
        res_ref[m] = h_ref[0, first + m]
    depth = []
    masks = edge_masks((batches * rows, chans), height, width)
    for layer in range(layers):
        g = h_ref[layer + 1, pl.ds(first, batches)].reshape(batches * rows, chans)
        back = lax.dot_general(
            g, w_ref[layer], (((1,), (1,)), ((), ())), preferred_element_type=jnp.float32
        )
        zed = z_ref[layer]
        sig = jax.nn.sigmoid(zed)
        dzed = back * sig * (1.0 + zed * (1.0 - sig))
        point = lax.dot_general(
            a_ref[layer], g, (((0,), (0,)), ((), ())), preferred_element_type=jnp.float32
        )
        point = point * scale
        for d in range(replicas):
            send_ref[d, layer * share : (layer + 1) * share, :] = point[
                d * share : (d + 1) * share
            ].astype(jnp.bfloat16)
        xf = xs_ref[layer].astype(jnp.float32)
        rows_out = []
        for tap, moved in shifted_taps(xf, masks, width, 1):
            rows_out.append(jnp.sum(moved * dzed, axis=0, keepdims=True))
        rows_out.append(jnp.zeros((pad_taps - taps, chans), jnp.float32))
        depth.append(jnp.concatenate(rows_out, axis=0) * scale)
    lane = lax.broadcasted_iota(jnp.int32, (pad_taps, chans), 1)
    for d in range(replicas):
        slot = jnp.zeros((pad_taps, chans), jnp.float32)
        for layer in range(layers):
            amount = (layer * share - d * share) % chans
            moved = depth[layer] if amount == 0 else pltpu.roll(depth[layer], amount, 1)
            keep = (lane >= layer * share) & (lane < (layer + 1) * share)
            slot = jnp.where(keep, moved, slot)
        send_ref[d, layers * share :, :] = slot.astype(jnp.bfloat16)


def body(section_inputs, grad_out, point_weights, depth_weights):
    sections = lax.axis_size("section")
    replicas = lax.axis_size("dp")
    my_section = lax.axis_index("section")
    batches = grad_out.shape[0]
    layers = point_weights.shape[1]
    chans = point_weights.shape[3]
    taps = depth_weights.shape[2]
    inputs = section_inputs[0]
    images, height, width = inputs.shape[1], inputs.shape[2], inputs.shape[3]
    rows = images * height * width
    weights = point_weights[0]
    kerns = depth_weights[0].astype(jnp.float32)
    vmem = pl.BlockSpec(memory_space=pltpu.VMEM)
    smem = pl.BlockSpec(memory_space=pltpu.SMEM)
    params = pltpu.CompilerParams(vmem_limit_bytes=VMEM_LIMIT)

    fwd_flops = 2 * layers * rows * chans * (chans + 3 * taps)
    fwd_cost = pl.CostEstimate(
        flops=fwd_flops,
        transcendentals=layers * rows * chans,
        bytes_accessed=2 * layers * chans * chans + 8 * layers * rows * chans,
    )
    top_all = grad_out.reshape(batches, rows, chans)
    x_all = inputs.reshape(batches, rows, chans)
    total_steps = batches + sections - 1
    buf_shapes = (
        jax.ShapeDtypeStruct((layers, batches, rows, chans), jnp.float32),
        jax.ShapeDtypeStruct((layers, batches, rows, chans), jnp.bfloat16),
        jax.ShapeDtypeStruct((layers, batches, rows, chans), jnp.bfloat16),
    )
    slot_spec = pl.BlockSpec((layers, None, rows, chans), lambda i, p: (0, p[0], 0, 0))
    fwd_in = [
        pl.BlockSpec((None, rows, chans), lambda i, p: (p[0], 0, 0)),
        pl.BlockSpec((layers, chans, chans), lambda i, p: (0, 0, 0)),
        pl.BlockSpec((layers, taps, chans), lambda i, p: (0, 0, 0)),
    ]

    def picked_at(step):
        batch_id = step - (sections - 1) + my_section
        valid = ((batch_id >= 0) & (batch_id < batches)).astype(jnp.int32)
        return jnp.clip(batch_id, 0, batches - 1), valid

    picked, _ = picked_at(0)
    zbuf, abuf, xbuf, hbuf = pl.pallas_call(
        functools.partial(fwd_first_kernel, height=height, width=width),
        out_shape=buf_shapes
        + (jax.ShapeDtypeStruct((layers + 1, total_steps, rows, chans), jnp.bfloat16),),
        grid_spec=pltpu.PrefetchScalarGridSpec(
            num_scalar_prefetch=1,
            grid=(1,),
            in_specs=fwd_in,
            out_specs=[slot_spec, slot_spec, slot_spec, pl.BlockSpec(memory_space=pl.ANY)],
        ),
        compiler_params=params,
        cost_estimate=fwd_cost,
    )(jnp.reshape(picked, (1,)).astype(jnp.int32), x_all, weights, kerns)

    carried = jnp.zeros((rows, chans), jnp.bfloat16)
    is_last = (my_section == sections - 1).astype(jnp.int32)
    for step in range(total_steps):
        picked, valid = picked_at(step)
        scalars = jnp.stack([picked, is_last, valid]).astype(jnp.int32)
        grid_spec = pltpu.PrefetchScalarGridSpec(
            num_scalar_prefetch=1,
            grid=(1,),
            in_specs=[
                pl.BlockSpec((None, rows, chans), lambda i, p: (p[0], 0, 0)),
                pl.BlockSpec((rows, chans), lambda i, p: (0, 0)),
                pl.BlockSpec((layers, None, rows, chans), lambda i, p: (0, p[0], 0, 0)),
                pl.BlockSpec((layers, chans, chans), lambda i, p: (0, 0, 0)),
                pl.BlockSpec((layers, taps, chans), lambda i, p: (0, 0, 0)),
                pl.BlockSpec(memory_space=pl.ANY),
            ],
            out_specs=[
                pl.BlockSpec((rows, chans), lambda i, p: (0, 0)),
                pl.BlockSpec(
                    (layers + 1, None, rows, chans), lambda i, p, s=step: (0, s, 0, 0)
                ),
            ],
        )
        g, hbuf = pl.pallas_call(
            functools.partial(step_kernel, height=height, width=width),
            out_shape=(
                jax.ShapeDtypeStruct((rows, chans), jnp.bfloat16),
                jax.ShapeDtypeStruct(hbuf.shape, jnp.bfloat16),
            ),
            grid_spec=grid_spec,
            input_output_aliases={6: 1},
            compiler_params=params,
            cost_estimate=fwd_cost,
        )(scalars, top_all, carried, zbuf, weights, kerns, hbuf)
        if step < total_steps - 1:
            carried = from_behind(g, "section", -1)
            nxt, _ = picked_at(step + 1)
            zbuf, abuf, xbuf = pl.pallas_call(
                functools.partial(fwd_kernel, height=height, width=width),
                out_shape=buf_shapes,
                grid_spec=pltpu.PrefetchScalarGridSpec(
                    num_scalar_prefetch=1,
                    grid=(1,),
                    in_specs=fwd_in + [pl.BlockSpec(memory_space=pl.ANY)] * 3,
                    out_specs=[slot_spec, slot_spec, slot_spec],
                ),
                input_output_aliases={4: 0, 5: 1, 6: 2},
                compiler_params=params,
                cost_estimate=fwd_cost,
            )(jnp.reshape(nxt, (1,)).astype(jnp.int32), x_all, weights, kerns, zbuf, abuf, xbuf)
    zs = zbuf.reshape(layers, batches * rows, chans)
    acts = abuf.reshape(layers, batches * rows, chans)
    xs = xbuf.reshape(layers, batches * rows, chans)

    count = batches * images * replicas * height * width
    scale = 1.0 / float(count) ** 0.5
    share = chans // replicas
    pad_taps = -(-taps // 16) * 16
    first = jnp.reshape(sections - 1 - my_section, (1,)).astype(jnp.int32)
    send, res = pl.pallas_call(
        functools.partial(grad_kernel, height=height, width=width, scale=scale),
        out_shape=(
            jax.ShapeDtypeStruct((replicas, layers * share + pad_taps, chans), jnp.bfloat16),
            jax.ShapeDtypeStruct((batches, rows, chans), jnp.bfloat16),
        ),
        in_specs=[smem, vmem, vmem, vmem, vmem, vmem, vmem],
        out_specs=(vmem, vmem),
        compiler_params=params,
    )(first, hbuf, acts, xs, zs, weights, kerns)
    recv = lax.all_to_all(send, "dp", 0, 0, tiled=True)
    summed = jnp.sum(recv.astype(jnp.float32), axis=0)
    point_red = summed[: layers * share].reshape(layers, share, chans)
    depth_red = summed[layers * share : layers * share + taps, : layers * share]
    depth_red = depth_red.reshape(taps, layers, share).transpose(1, 0, 2)
    results = res.reshape(inputs.shape)
    return (results[None], point_red[None], depth_red[None])


def solution(mesh):
    return jax.shard_map(
        body,
        mesh=mesh,
        in_specs=(
            P("section", None, "dp", None, None, None),
            P(None, "dp", None, None, None),
            P("section", None, None, None),
            P("section", None, None, None),
        ),
        out_specs=(
            P("section", None, "dp", None, None, None),
            P("section", None, "dp", None),
            P("section", None, None, "dp"),
        ),
        check_vma=False,
    )
```

```python
import functools

import jax
import jax.numpy as jnp
from jax import lax
from jax.experimental import pallas as pl
from jax.experimental.pallas import tpu as pltpu
from jax.sharding import PartitionSpec as P

VMEM_LIMIT = 60 * 1024 * 1024


def from_behind(shard, axis, by):
    devices = lax.axis_size(axis)
    pairs = [(i, i + by) for i in range(devices) if 0 <= i + by < devices]
    return lax.ppermute(shard, axis, pairs)


def shift_rows(x, off):
    rows = x.shape[0]
    amount = (-off) % rows
    return x if amount == 0 else pltpu.roll(x, amount, 0)


def edge_masks(shape, height, width):
    r = lax.broadcasted_iota(jnp.int32, shape, 0)
    if width & (width - 1) == 0 and height & (height - 1) == 0:
        j = r & (width - 1)
        i = lax.shift_right_logical(r, width.bit_length() - 1) & (height - 1)
    else:
        j = lax.rem(r, width)
        i = lax.rem(lax.div(r, width), height)
    return {
        ("i", -1): i >= 1,
        ("i", 1): i < height - 1,
        ("j", -1): j >= 1,
        ("j", 1): j < width - 1,
    }


def offsets():
    for di in (-1, 0, 1):
        for dj in (-1, 0, 1):
            yield 3 * (di + 1) + (dj + 1), di, dj


def shifted_taps(x, masks, width, sign):
    cols = {}
    for dj in (-1, 0, 1):
        s = sign * dj
        cols[dj] = x if s == 0 else jnp.where(masks[("j", s)], shift_rows(x, s), 0.0)
    for tap, di, dj in offsets():
        s = sign * di
        c = cols[dj]
        yield tap, (c if s == 0 else jnp.where(masks[("i", s)], shift_rows(c, s * width), 0.0))


def stencil(x, k_ref, layer, masks, width, sign):
    total = jnp.zeros(x.shape, jnp.float32)
    for tap, moved in shifted_taps(x, masks, width, sign):
        total = total + k_ref[layer, tap : tap + 1, :] * moved
    return total


def fwd_kernel(p_ref, x_ref, w_ref, k_ref, *refs, height, width):
    z_ref, a_ref, xs_ref = refs[-3:]
    layers = w_ref.shape[0]
    field = x_ref[...]
    masks = edge_masks(field.shape, height, width)
    for layer in range(layers):
        xs_ref[layer] = field
        xf = field.astype(jnp.float32)
        zed = stencil(xf, k_ref, layer, masks, width, 1)
        z_ref[layer] = zed
        act = (zed * jax.nn.sigmoid(zed)).astype(jnp.bfloat16)
        a_ref[layer] = act
        branch = jnp.dot(act, w_ref[layer], preferred_element_type=jnp.float32)
        field = (xf + branch).astype(jnp.bfloat16)


def fwd_first_kernel(p_ref, x_ref, w_ref, k_ref, z_ref, a_ref, xs_ref, h_ref, *, height, width):
    del h_ref
    fwd_kernel(p_ref, x_ref, w_ref, k_ref, z_ref, a_ref, xs_ref, height=height, width=width)


def step_kernel(
    p_ref, top_ref, car_ref, z_ref, w_ref, k_ref, h_in, g_ref, h_ref, *, height, width, step
):
    del h_in
    layers = w_ref.shape[0]
    top = top_ref[...].astype(jnp.float32)
    car = car_ref[...].astype(jnp.float32)
    g = jnp.where(p_ref[step, 1] == 1, top, car)
    g = jnp.where(p_ref[step, 2] == 1, g, 0.0).astype(jnp.bfloat16)
    h_ref[layers] = g
    masks = edge_masks(g.shape, height, width)
    for layer in reversed(range(layers)):
        back = lax.dot_general(
            g, w_ref[layer], (((1,), (1,)), ((), ())), preferred_element_type=jnp.float32
        )
        zed = z_ref[layer]
        sig = jax.nn.sigmoid(zed)
        dzed = back * sig * (1.0 + zed * (1.0 - sig))
        g = (g.astype(jnp.float32) + stencil(dzed, k_ref, layer, masks, width, -1)).astype(
            jnp.bfloat16
        )
        h_ref[layer] = g
    g_ref[...] = g


def grad_kernel(
    p_ref, h_ref, a_ref, xs_ref, z_ref, w_ref, k_ref, send_ref, res_ref, *, height, width, scale
):
    layers, chans = w_ref.shape[0], w_ref.shape[2]
    taps = k_ref.shape[1]
    batches = res_ref.shape[0]
    rows = h_ref.shape[2]
    replicas = send_ref.shape[0]
    share = chans // replicas
    pad_taps = send_ref.shape[1] - layers * share
    first = p_ref[0]
    for m in range(batches):
        res_ref[m] = h_ref[0, first + m]
    depth = []
    masks = edge_masks((batches * rows, chans), height, width)
    for layer in range(layers):
        g = h_ref[layer + 1, pl.ds(first, batches)].reshape(batches * rows, chans)
        back = lax.dot_general(
            g, w_ref[layer], (((1,), (1,)), ((), ())), preferred_element_type=jnp.float32
        )
        zed = z_ref[layer]
        sig = jax.nn.sigmoid(zed)
        dzed = back * sig * (1.0 + zed * (1.0 - sig))
        point = lax.dot_general(
            a_ref[layer], g, (((0,), (0,)), ((), ())), preferred_element_type=jnp.float32
        )
        point = point * scale
        for d in range(replicas):
            send_ref[d, layer * share : (layer + 1) * share, :] = point[
                d * share : (d + 1) * share
            ].astype(jnp.bfloat16)
        xf = xs_ref[layer].astype(jnp.float32)
        rows_out = []
        for tap, moved in shifted_taps(xf, masks, width, 1):
            rows_out.append(jnp.sum(moved * dzed, axis=0, keepdims=True))
        rows_out.append(jnp.zeros((pad_taps - taps, chans), jnp.float32))
        depth.append(jnp.concatenate(rows_out, axis=0) * scale)
    lane = lax.broadcasted_iota(jnp.int32, (pad_taps, chans), 1)
    for d in range(replicas):
        slot = jnp.zeros((pad_taps, chans), jnp.float32)
        for layer in range(layers):
            amount = (layer * share - d * share) % chans
            moved = depth[layer] if amount == 0 else pltpu.roll(depth[layer], amount, 1)
            keep = (lane >= layer * share) & (lane < (layer + 1) * share)
            slot = jnp.where(keep, moved, slot)
        send_ref[d, layers * share :, :] = slot.astype(jnp.bfloat16)


def body(section_inputs, grad_out, point_weights, depth_weights):
    sections = lax.axis_size("section")
    replicas = lax.axis_size("dp")
    my_section = lax.axis_index("section")
    batches = grad_out.shape[0]
    layers = point_weights.shape[1]
    chans = point_weights.shape[3]
    taps = depth_weights.shape[2]
    inputs = section_inputs[0]
    images, height, width = inputs.shape[1], inputs.shape[2], inputs.shape[3]
    rows = images * height * width
    weights = point_weights[0]
    kerns = depth_weights[0].astype(jnp.float32)
    vmem = pl.BlockSpec(memory_space=pltpu.VMEM)
    smem = pl.BlockSpec(memory_space=pltpu.SMEM)
    params = pltpu.CompilerParams(vmem_limit_bytes=VMEM_LIMIT)

    fwd_flops = 2 * layers * rows * chans * (chans + 3 * taps)
    fwd_cost = pl.CostEstimate(
        flops=fwd_flops,
        transcendentals=layers * rows * chans,
        bytes_accessed=2 * layers * chans * chans + 8 * layers * rows * chans,
    )
    top_all = grad_out.reshape(batches, rows, chans)
    x_all = inputs.reshape(batches, rows, chans)
    total_steps = batches + sections - 1
    buf_shapes = (
        jax.ShapeDtypeStruct((layers, batches, rows, chans), jnp.float32),
        jax.ShapeDtypeStruct((layers, batches, rows, chans), jnp.bfloat16),
        jax.ShapeDtypeStruct((layers, batches, rows, chans), jnp.bfloat16),
    )

    def slot_spec(step):
        return pl.BlockSpec((layers, None, rows, chans), lambda i, p, s=step: (0, p[s, 0], 0, 0))

    def fwd_in(step):
        return [
            pl.BlockSpec((None, rows, chans), lambda i, p, s=step: (p[s, 0], 0, 0)),
            pl.BlockSpec((layers, chans, chans), lambda i, p: (0, 0, 0)),
            pl.BlockSpec((layers, taps, chans), lambda i, p: (0, 0, 0)),
        ]

    def picked_at(step):
        batch_id = step - (sections - 1) + my_section
        valid = ((batch_id >= 0) & (batch_id < batches)).astype(jnp.int32)
        return jnp.clip(batch_id, 0, batches - 1), valid

    is_last = (my_section == sections - 1).astype(jnp.int32)
    table = jnp.stack(
        [jnp.stack([picked_at(s)[0], is_last, picked_at(s)[1]]) for s in range(total_steps)]
    ).astype(jnp.int32)
    zbuf, abuf, xbuf, hbuf = pl.pallas_call(
        functools.partial(fwd_first_kernel, height=height, width=width),
        out_shape=buf_shapes
        + (jax.ShapeDtypeStruct((layers + 1, total_steps, rows, chans), jnp.bfloat16),),
        grid_spec=pltpu.PrefetchScalarGridSpec(
            num_scalar_prefetch=1,
            grid=(1,),
            in_specs=fwd_in(0),
            out_specs=[slot_spec(0)] * 3 + [pl.BlockSpec(memory_space=pl.ANY)],
        ),
        compiler_params=params,
        cost_estimate=fwd_cost,
    )(table, x_all, weights, kerns)

    carried = jnp.zeros((rows, chans), jnp.bfloat16)
    for step in range(total_steps):
        grid_spec = pltpu.PrefetchScalarGridSpec(
            num_scalar_prefetch=1,
            grid=(1,),
            in_specs=[
                pl.BlockSpec((None, rows, chans), lambda i, p, s=step: (p[s, 0], 0, 0)),
                pl.BlockSpec(memory_space=pltpu.VMEM),
                slot_spec(step),
                pl.BlockSpec((layers, chans, chans), lambda i, p: (0, 0, 0)),
                pl.BlockSpec((layers, taps, chans), lambda i, p: (0, 0, 0)),
                pl.BlockSpec(memory_space=pl.ANY),
            ],
            out_specs=[
                pl.BlockSpec((rows, chans), lambda i, p: (0, 0)),
                pl.BlockSpec(
                    (layers + 1, None, rows, chans), lambda i, p, s=step: (0, s, 0, 0)
                ),
            ],
        )
        g, hbuf = pl.pallas_call(
            functools.partial(step_kernel, height=height, width=width, step=step),
            out_shape=(
                jax.ShapeDtypeStruct((rows, chans), jnp.bfloat16),
                jax.ShapeDtypeStruct(hbuf.shape, jnp.bfloat16),
            ),
            grid_spec=grid_spec,
            input_output_aliases={6: 1},
            compiler_params=params,
            cost_estimate=fwd_cost,
        )(table, top_all, carried, zbuf, weights, kerns, hbuf)
        if step < total_steps - 1:
            carried = from_behind(g, "section", -1)
            zbuf, abuf, xbuf = pl.pallas_call(
                functools.partial(fwd_kernel, height=height, width=width),
                out_shape=buf_shapes,
                grid_spec=pltpu.PrefetchScalarGridSpec(
                    num_scalar_prefetch=1,
                    grid=(1,),
                    in_specs=fwd_in(step + 1) + [pl.BlockSpec(memory_space=pl.ANY)] * 3,
                    out_specs=[slot_spec(step + 1)] * 3,
                ),
                input_output_aliases={4: 0, 5: 1, 6: 2},
                compiler_params=params,
                cost_estimate=fwd_cost,
            )(table, x_all, weights, kerns, zbuf, abuf, xbuf)
    zs = zbuf.reshape(layers, batches * rows, chans)
    acts = abuf.reshape(layers, batches * rows, chans)
    xs = xbuf.reshape(layers, batches * rows, chans)

    count = batches * images * replicas * height * width
    scale = 1.0 / float(count) ** 0.5
    share = chans // replicas
    pad_taps = -(-taps // 16) * 16
    first = jnp.reshape(sections - 1 - my_section, (1,)).astype(jnp.int32)
    send, res = pl.pallas_call(
        functools.partial(grad_kernel, height=height, width=width, scale=scale),
        out_shape=(
            jax.ShapeDtypeStruct((replicas, layers * share + pad_taps, chans), jnp.bfloat16),
            jax.ShapeDtypeStruct((batches, rows, chans), jnp.bfloat16),
        ),
        in_specs=[smem, vmem, vmem, vmem, vmem, vmem, vmem],
        out_specs=(vmem, vmem),
        compiler_params=params,
    )(first, hbuf, acts, xs, zs, weights, kerns)
    recv = lax.all_to_all(send, "dp", 0, 0, tiled=True)
    summed = jnp.sum(recv.astype(jnp.float32), axis=0)
    point_red = summed[: layers * share].reshape(layers, share, chans)
    depth_red = summed[layers * share : layers * share + taps, : layers * share]
    depth_red = depth_red.reshape(taps, layers, share).transpose(1, 0, 2)
    results = res.reshape(inputs.shape)
    return (results[None], point_red[None], depth_red[None])


def solution(mesh):
    return jax.shard_map(
        body,
        mesh=mesh,
        in_specs=(
            P("section", None, "dp", None, None, None),
            P(None, "dp", None, None, None),
            P("section", None, None, None),
            P("section", None, None, None),
        ),
        out_specs=(
            P("section", None, "dp", None, None, None),
            P("section", None, "dp", None),
            P("section", None, None, "dp"),
        ),
        check_vma=False,
    )
```

```python
import functools

import jax
import jax.numpy as jnp
from jax import lax
from jax.experimental import pallas as pl
from jax.experimental.pallas import tpu as pltpu
from jax.sharding import Mesh, PartitionSpec as P

VMEM_LIMIT = 60 * 1024 * 1024


def from_behind(shard, axis, by):
    devices = lax.axis_size(axis)
    pairs = [(i, i + by) for i in range(devices) if 0 <= i + by < devices]
    return lax.ppermute(shard, axis, pairs)


def shift_rows(x, off):
    rows = x.shape[0]
    amount = (-off) % rows
    return x if amount == 0 else pltpu.roll(x, amount, 0)


def edge_masks(shape, height, width):
    r = lax.broadcasted_iota(jnp.int32, shape, 0)
    if width & (width - 1) == 0 and height & (height - 1) == 0:
        j = r & (width - 1)
        i = lax.shift_right_logical(r, width.bit_length() - 1) & (height - 1)
    else:
        j = lax.rem(r, width)
        i = lax.rem(lax.div(r, width), height)
    return {
        ("i", -1): i >= 1,
        ("i", 1): i < height - 1,
        ("j", -1): j >= 1,
        ("j", 1): j < width - 1,
    }


def offsets():
    for di in (-1, 0, 1):
        for dj in (-1, 0, 1):
            yield 3 * (di + 1) + (dj + 1), di, dj


def shifted_taps(x, masks, width, sign):
    cols = {}
    for dj in (-1, 0, 1):
        s = sign * dj
        cols[dj] = x if s == 0 else jnp.where(masks[("j", s)], shift_rows(x, s), 0.0)
    for tap, di, dj in offsets():
        s = sign * di
        c = cols[dj]
        yield tap, (c if s == 0 else jnp.where(masks[("i", s)], shift_rows(c, s * width), 0.0))


def stencil(x, k_ref, layer, masks, width, sign):
    total = jnp.zeros(x.shape, jnp.float32)
    for tap, moved in shifted_taps(x, masks, width, sign):
        total = total + k_ref[layer, tap : tap + 1, :] * moved
    return total


def fwd_kernel(p_ref, x_ref, w_ref, k_ref, *refs, height, width):
    z_ref, a_ref, xs_ref = refs[-3:]
    layers = w_ref.shape[0]
    field = x_ref[...]
    masks = edge_masks(field.shape, height, width)
    for layer in range(layers):
        xs_ref[layer] = field
        xf = field.astype(jnp.float32)
        zed = stencil(xf, k_ref, layer, masks, width, 1)
        z_ref[layer] = zed
        act = (zed * jax.nn.sigmoid(zed)).astype(jnp.bfloat16)
        a_ref[layer] = act
        branch = jnp.dot(act, w_ref[layer], preferred_element_type=jnp.float32)
        field = (xf + branch).astype(jnp.bfloat16)


def fwd_first_kernel(p_ref, x_ref, w_ref, k_ref, z_ref, a_ref, xs_ref, h_ref, *, height, width):
    del h_ref
    fwd_kernel(p_ref, x_ref, w_ref, k_ref, z_ref, a_ref, xs_ref, height=height, width=width)


def step_kernel(p_ref, top_ref, car_ref, z_ref, w_ref, k_ref, h_in, g_ref, h_ref, *, height, width):
    del h_in
    layers = w_ref.shape[0]
    top = top_ref[...].astype(jnp.float32)
    car = car_ref[...].astype(jnp.float32)
    g = jnp.where(p_ref[1] == 1, top, car)
    g = jnp.where(p_ref[2] == 1, g, 0.0).astype(jnp.bfloat16)
    h_ref[layers] = g
    masks = edge_masks(g.shape, height, width)
    for layer in reversed(range(layers)):
        back = lax.dot_general(
            g, w_ref[layer], (((1,), (1,)), ((), ())), preferred_element_type=jnp.float32
        )
        zed = z_ref[layer]
        sig = jax.nn.sigmoid(zed)
        dzed = back * sig * (1.0 + zed * (1.0 - sig))
        g = (g.astype(jnp.float32) + stencil(dzed, k_ref, layer, masks, width, -1)).astype(
            jnp.bfloat16
        )
        h_ref[layer] = g
    g_ref[...] = g


def grad_kernel(
    p_ref, h_ref, a_ref, xs_ref, z_ref, w_ref, k_ref, send_ref, res_ref, *, height, width, scale
):
    layers, chans = w_ref.shape[0], w_ref.shape[2]
    taps = k_ref.shape[1]
    batches = res_ref.shape[0]
    rows = h_ref.shape[2]
    replicas = send_ref.shape[0]
    share = chans // replicas
    pad_taps = send_ref.shape[1] - layers * share
    first = p_ref[0]
    for m in range(batches):
        res_ref[m] = h_ref[0, first + m]
    depth = []
    masks = edge_masks((batches * rows, chans), height, width)
    for layer in range(layers):
        g = h_ref[layer + 1, pl.ds(first, batches)].reshape(batches * rows, chans)
        back = lax.dot_general(
            g, w_ref[layer], (((1,), (1,)), ((), ())), preferred_element_type=jnp.float32
        )
        zed = z_ref[layer]
        sig = jax.nn.sigmoid(zed)
        dzed = back * sig * (1.0 + zed * (1.0 - sig))
        point = lax.dot_general(
            a_ref[layer], g, (((0,), (0,)), ((), ())), preferred_element_type=jnp.float32
        )
        point = point * scale
        for d in range(replicas):
            send_ref[d, layer * share : (layer + 1) * share, :] = point[
                d * share : (d + 1) * share
            ].astype(jnp.bfloat16)
        xf = xs_ref[layer].astype(jnp.float32)
        rows_out = []
        for tap, moved in shifted_taps(xf, masks, width, 1):
            rows_out.append(jnp.sum(moved * dzed, axis=0, keepdims=True))
        rows_out.append(jnp.zeros((pad_taps - taps, chans), jnp.float32))
        depth.append(jnp.concatenate(rows_out, axis=0) * scale)
    lane = lax.broadcasted_iota(jnp.int32, (pad_taps, chans), 1)
    for d in range(replicas):
        slot = jnp.zeros((pad_taps, chans), jnp.float32)
        for layer in range(layers):
            amount = (layer * share - d * share) % chans
            moved = depth[layer] if amount == 0 else pltpu.roll(depth[layer], amount, 1)
            keep = (lane >= layer * share) & (lane < (layer + 1) * share)
            slot = jnp.where(keep, moved, slot)
        send_ref[d, layers * share :, :] = slot.astype(jnp.bfloat16)


def body(section_inputs, grad_out, point_weights, depth_weights):
    sections = lax.axis_size("section")
    replicas = lax.axis_size("chip") * lax.axis_size("core")
    my_section = lax.axis_index("section")
    batches = grad_out.shape[0]
    layers = point_weights.shape[1]
    chans = point_weights.shape[3]
    taps = depth_weights.shape[2]
    inputs = section_inputs[0]
    images, height, width = inputs.shape[1], inputs.shape[2], inputs.shape[3]
    rows = images * height * width
    weights = point_weights[0]
    kerns = depth_weights[0].astype(jnp.float32)
    vmem = pl.BlockSpec(memory_space=pltpu.VMEM)
    smem = pl.BlockSpec(memory_space=pltpu.SMEM)
    params = pltpu.CompilerParams(vmem_limit_bytes=VMEM_LIMIT)

    fwd_flops = 2 * layers * rows * chans * (chans + 3 * taps)
    fwd_cost = pl.CostEstimate(
        flops=fwd_flops,
        transcendentals=layers * rows * chans,
        bytes_accessed=2 * layers * chans * chans + 8 * layers * rows * chans,
    )
    top_all = grad_out.reshape(batches, rows, chans)
    x_all = inputs.reshape(batches, rows, chans)
    total_steps = batches + sections - 1
    buf_shapes = (
        jax.ShapeDtypeStruct((layers, batches, rows, chans), jnp.float32),
        jax.ShapeDtypeStruct((layers, batches, rows, chans), jnp.bfloat16),
        jax.ShapeDtypeStruct((layers, batches, rows, chans), jnp.bfloat16),
    )
    slot_spec = pl.BlockSpec((layers, None, rows, chans), lambda i, p: (0, p[0], 0, 0))
    fwd_in = [
        pl.BlockSpec((None, rows, chans), lambda i, p: (p[0], 0, 0)),
        pl.BlockSpec((layers, chans, chans), lambda i, p: (0, 0, 0)),
        pl.BlockSpec((layers, taps, chans), lambda i, p: (0, 0, 0)),
    ]

    def picked_at(step):
        batch_id = step - (sections - 1) + my_section
        valid = ((batch_id >= 0) & (batch_id < batches)).astype(jnp.int32)
        return jnp.clip(batch_id, 0, batches - 1), valid

    picked, _ = picked_at(0)
    zbuf, abuf, xbuf, hbuf = pl.pallas_call(
        functools.partial(fwd_first_kernel, height=height, width=width),
        out_shape=buf_shapes
        + (jax.ShapeDtypeStruct((layers + 1, total_steps, rows, chans), jnp.bfloat16),),
        grid_spec=pltpu.PrefetchScalarGridSpec(
            num_scalar_prefetch=1,
            grid=(1,),
            in_specs=fwd_in,
            out_specs=[slot_spec, slot_spec, slot_spec, pl.BlockSpec(memory_space=pl.ANY)],
        ),
        compiler_params=params,
        cost_estimate=fwd_cost,
    )(jnp.reshape(picked, (1,)).astype(jnp.int32), x_all, weights, kerns)

    carried = jnp.zeros((rows, chans), jnp.bfloat16)
    is_last = (my_section == sections - 1).astype(jnp.int32)
    for step in range(total_steps):
        picked, valid = picked_at(step)
        scalars = jnp.stack([picked, is_last, valid]).astype(jnp.int32)
        grid_spec = pltpu.PrefetchScalarGridSpec(
            num_scalar_prefetch=1,
            grid=(1,),
            in_specs=[
                pl.BlockSpec((None, rows, chans), lambda i, p: (p[0], 0, 0)),
                pl.BlockSpec((rows, chans), lambda i, p: (0, 0)),
                pl.BlockSpec((layers, None, rows, chans), lambda i, p: (0, p[0], 0, 0)),
                pl.BlockSpec((layers, chans, chans), lambda i, p: (0, 0, 0)),
                pl.BlockSpec((layers, taps, chans), lambda i, p: (0, 0, 0)),
                pl.BlockSpec(memory_space=pl.ANY),
            ],
            out_specs=[
                pl.BlockSpec((rows, chans), lambda i, p: (0, 0)),
                pl.BlockSpec(
                    (layers + 1, None, rows, chans), lambda i, p, s=step: (0, s, 0, 0)
                ),
            ],
        )
        g, hbuf = pl.pallas_call(
            functools.partial(step_kernel, height=height, width=width),
            out_shape=(
                jax.ShapeDtypeStruct((rows, chans), jnp.bfloat16),
                jax.ShapeDtypeStruct(hbuf.shape, jnp.bfloat16),
            ),
            grid_spec=grid_spec,
            input_output_aliases={6: 1},
            compiler_params=params,
            cost_estimate=fwd_cost,
        )(scalars, top_all, carried, zbuf, weights, kerns, hbuf)
        if step < total_steps - 1:
            carried = from_behind(g, "section", -1)
            nxt, _ = picked_at(step + 1)
            zbuf, abuf, xbuf = pl.pallas_call(
                functools.partial(fwd_kernel, height=height, width=width),
                out_shape=buf_shapes,
                grid_spec=pltpu.PrefetchScalarGridSpec(
                    num_scalar_prefetch=1,
                    grid=(1,),
                    in_specs=fwd_in + [pl.BlockSpec(memory_space=pl.ANY)] * 3,
                    out_specs=[slot_spec, slot_spec, slot_spec],
                ),
                input_output_aliases={4: 0, 5: 1, 6: 2},
                compiler_params=params,
                cost_estimate=fwd_cost,
            )(jnp.reshape(nxt, (1,)).astype(jnp.int32), x_all, weights, kerns, zbuf, abuf, xbuf)
    zs = zbuf.reshape(layers, batches * rows, chans)
    acts = abuf.reshape(layers, batches * rows, chans)
    xs = xbuf.reshape(layers, batches * rows, chans)

    count = batches * images * replicas * height * width
    scale = 1.0 / float(count) ** 0.5
    share = chans // replicas
    pad_taps = -(-taps // 16) * 16
    first = jnp.reshape(sections - 1 - my_section, (1,)).astype(jnp.int32)
    send, res = pl.pallas_call(
        functools.partial(grad_kernel, height=height, width=width, scale=scale),
        out_shape=(
            jax.ShapeDtypeStruct((replicas, layers * share + pad_taps, chans), jnp.bfloat16),
            jax.ShapeDtypeStruct((batches, rows, chans), jnp.bfloat16),
        ),
        in_specs=[smem, vmem, vmem, vmem, vmem, vmem, vmem],
        out_specs=(vmem, vmem),
        compiler_params=params,
    )(first, hbuf, acts, xs, zs, weights, kerns)
    cores = lax.axis_size("core")
    send = send.reshape((replicas // cores, cores) + send.shape[1:])
    pair = lax.all_to_all(send, "core", 1, 1, tiled=True)
    pair = jnp.sum(pair.astype(jnp.float32), axis=1).astype(jnp.bfloat16)
    recv = lax.all_to_all(pair, "chip", 0, 0, tiled=True)
    summed = jnp.sum(recv.astype(jnp.float32), axis=0)
    point_red = summed[: layers * share].reshape(layers, share, chans)
    depth_red = summed[layers * share : layers * share + taps, : layers * share]
    depth_red = depth_red.reshape(taps, layers, share).transpose(1, 0, 2)
    results = res.reshape(inputs.shape)
    return (results[None], point_red[None], depth_red[None])


def solution(mesh):
    sections, replicas = mesh.devices.shape
    split = Mesh(mesh.devices.reshape(sections, replicas // 2, 2), ("section", "chip", "core"))
    dp = ("chip", "core")
    return jax.shard_map(
        body,
        mesh=split,
        in_specs=(
            P("section", None, dp, None, None, None),
            P(None, dp, None, None, None),
            P("section", None, None, None),
            P("section", None, None, None),
        ),
        out_specs=(
            P("section", None, dp, None, None, None),
            P("section", None, dp, None),
            P("section", None, None, dp),
        ),
        check_vma=False,
    )
```

```python
import functools
import math

import jax
import numpy as np
import jax.numpy as jnp
from jax import lax
from jax.experimental import pallas as pl
from jax.experimental.pallas import tpu as pltpu
from jax.sharding import Mesh, PartitionSpec as P

VMEM_LIMIT = 60 * 1024 * 1024


def from_behind(shard, axis, by):
    devices = lax.axis_size(axis)
    pairs = [(i, i + by) for i in range(devices) if 0 <= i + by < devices]
    return lax.ppermute(shard, axis, pairs)


def shift_rows(x, off):
    rows = x.shape[0]
    amount = (-off) % rows
    return x if amount == 0 else pltpu.roll(x, amount, 0)


def edge_masks(shape, height, width):
    r = lax.broadcasted_iota(jnp.int32, shape, 0)
    if width & (width - 1) == 0 and height & (height - 1) == 0:
        j = r & (width - 1)
        i = lax.shift_right_logical(r, width.bit_length() - 1) & (height - 1)
    else:
        j = lax.rem(r, width)
        i = lax.rem(lax.div(r, width), height)
    return {
        ("i", -1): i >= 1,
        ("i", 1): i < height - 1,
        ("j", -1): j >= 1,
        ("j", 1): j < width - 1,
    }


def offsets():
    for di in (-1, 0, 1):
        for dj in (-1, 0, 1):
            yield 3 * (di + 1) + (dj + 1), di, dj


def shifted_taps(x, masks, width, sign):
    cols = {}
    for dj in (-1, 0, 1):
        s = sign * dj
        cols[dj] = x if s == 0 else jnp.where(masks[("j", s)], shift_rows(x, s), 0.0)
    for tap, di, dj in offsets():
        s = sign * di
        c = cols[dj]
        yield tap, (c if s == 0 else jnp.where(masks[("i", s)], shift_rows(c, s * width), 0.0))


def stencil(x, k_ref, layer, masks, width, sign):
    total = jnp.zeros(x.shape, jnp.float32)
    for tap, moved in shifted_taps(x, masks, width, sign):
        total = total + k_ref[layer, tap : tap + 1, :] * moved
    return total


def fwd_kernel(p_ref, x_ref, w_ref, k_ref, *refs, height, width):
    z_ref, a_ref, xs_ref = refs[-3:]
    layers = w_ref.shape[0]
    field = x_ref[...]
    masks = edge_masks(field.shape, height, width)
    for layer in range(layers):
        xs_ref[layer] = field
        xf = field.astype(jnp.float32)
        zed = stencil(xf, k_ref, layer, masks, width, 1)
        z_ref[layer] = zed
        act = (zed * jax.nn.sigmoid(zed)).astype(jnp.bfloat16)
        a_ref[layer] = act
        branch = jnp.dot(act, w_ref[layer], preferred_element_type=jnp.float32)
        field = (xf + branch).astype(jnp.bfloat16)


def fwd_first_kernel(p_ref, x_ref, w_ref, k_ref, z_ref, a_ref, xs_ref, h_ref, *, height, width):
    del h_ref
    fwd_kernel(p_ref, x_ref, w_ref, k_ref, z_ref, a_ref, xs_ref, height=height, width=width)


def step_kernel(p_ref, top_ref, car_ref, z_ref, w_ref, k_ref, h_in, g_ref, h_ref, *, height, width):
    del h_in
    layers = w_ref.shape[0]
    top = top_ref[...].astype(jnp.float32)
    car = car_ref[...].astype(jnp.float32)
    g = jnp.where(p_ref[1] == 1, top, car)
    g = jnp.where(p_ref[2] == 1, g, 0.0).astype(jnp.bfloat16)
    h_ref[layers] = g
    masks = edge_masks(g.shape, height, width)
    for layer in reversed(range(layers)):
        back = lax.dot_general(
            g, w_ref[layer], (((1,), (1,)), ((), ())), preferred_element_type=jnp.float32
        )
        zed = z_ref[layer]
        sig = jax.nn.sigmoid(zed)
        dzed = back * sig * (1.0 + zed * (1.0 - sig))
        g = (g.astype(jnp.float32) + stencil(dzed, k_ref, layer, masks, width, -1)).astype(
            jnp.bfloat16
        )
        h_ref[layer] = g
    g_ref[...] = g


def grad_kernel(
    p_ref, h_ref, a_ref, xs_ref, z_ref, w_ref, k_ref, send_ref, res_ref, *, height, width, scale
):
    layers, chans = w_ref.shape[0], w_ref.shape[2]
    taps = k_ref.shape[1]
    batches = res_ref.shape[0]
    rows = h_ref.shape[2]
    lead = send_ref.shape[:-2]
    replicas = math.prod(lead)
    share = chans // replicas
    pad_taps = send_ref.shape[-2] - layers * share
    first = p_ref[0]
    for m in range(batches):
        res_ref[m] = h_ref[0, first + m]
    depth = []
    masks = edge_masks((batches * rows, chans), height, width)
    for layer in range(layers):
        g = h_ref[layer + 1, pl.ds(first, batches)].reshape(batches * rows, chans)
        back = lax.dot_general(
            g, w_ref[layer], (((1,), (1,)), ((), ())), preferred_element_type=jnp.float32
        )
        zed = z_ref[layer]
        sig = jax.nn.sigmoid(zed)
        dzed = back * sig * (1.0 + zed * (1.0 - sig))
        point = lax.dot_general(
            a_ref[layer], g, (((0,), (0,)), ((), ())), preferred_element_type=jnp.float32
        )
        point = point * scale
        for d in range(replicas):
            send_ref[np.unravel_index(d, lead) + (slice(layer * share, (layer + 1) * share),)] = point[
                d * share : (d + 1) * share
            ].astype(jnp.bfloat16)
        xf = xs_ref[layer].astype(jnp.float32)
        rows_out = []
        for tap, moved in shifted_taps(xf, masks, width, 1):
            rows_out.append(jnp.sum(moved * dzed, axis=0, keepdims=True))
        rows_out.append(jnp.zeros((pad_taps - taps, chans), jnp.float32))
        depth.append(jnp.concatenate(rows_out, axis=0) * scale)
    lane = lax.broadcasted_iota(jnp.int32, (pad_taps, chans), 1)
    for d in range(replicas):
        slot = jnp.zeros((pad_taps, chans), jnp.float32)
        for layer in range(layers):
            amount = (layer * share - d * share) % chans
            moved = depth[layer] if amount == 0 else pltpu.roll(depth[layer], amount, 1)
            keep = (lane >= layer * share) & (lane < (layer + 1) * share)
            slot = jnp.where(keep, moved, slot)
        send_ref[np.unravel_index(d, lead) + (slice(layers * share, None),)] = slot.astype(
            jnp.bfloat16
        )


def body(section_inputs, grad_out, point_weights, depth_weights):
    sections = lax.axis_size("section")
    lead = (lax.axis_size("y"), lax.axis_size("z"), lax.axis_size("core"))
    replicas = math.prod(lead)
    my_section = lax.axis_index("section")
    batches = grad_out.shape[0]
    layers = point_weights.shape[1]
    chans = point_weights.shape[3]
    taps = depth_weights.shape[2]
    inputs = section_inputs[0]
    images, height, width = inputs.shape[1], inputs.shape[2], inputs.shape[3]
    rows = images * height * width
    weights = point_weights[0]
    kerns = depth_weights[0].astype(jnp.float32)
    vmem = pl.BlockSpec(memory_space=pltpu.VMEM)
    smem = pl.BlockSpec(memory_space=pltpu.SMEM)
    params = pltpu.CompilerParams(vmem_limit_bytes=VMEM_LIMIT)

    fwd_flops = 2 * layers * rows * chans * (chans + 3 * taps)
    fwd_cost = pl.CostEstimate(
        flops=fwd_flops,
        transcendentals=layers * rows * chans,
        bytes_accessed=2 * layers * chans * chans + 8 * layers * rows * chans,
    )
    top_all = grad_out.reshape(batches, rows, chans)
    x_all = inputs.reshape(batches, rows, chans)
    total_steps = batches + sections - 1
    buf_shapes = (
        jax.ShapeDtypeStruct((layers, batches, rows, chans), jnp.float32),
        jax.ShapeDtypeStruct((layers, batches, rows, chans), jnp.bfloat16),
        jax.ShapeDtypeStruct((layers, batches, rows, chans), jnp.bfloat16),
    )
    slot_spec = pl.BlockSpec((layers, None, rows, chans), lambda i, p: (0, p[0], 0, 0))
    fwd_in = [
        pl.BlockSpec((None, rows, chans), lambda i, p: (p[0], 0, 0)),
        pl.BlockSpec((layers, chans, chans), lambda i, p: (0, 0, 0)),
        pl.BlockSpec((layers, taps, chans), lambda i, p: (0, 0, 0)),
    ]

    def picked_at(step):
        batch_id = step - (sections - 1) + my_section
        valid = ((batch_id >= 0) & (batch_id < batches)).astype(jnp.int32)
        return jnp.clip(batch_id, 0, batches - 1), valid

    picked, _ = picked_at(0)
    zbuf, abuf, xbuf, hbuf = pl.pallas_call(
        functools.partial(fwd_first_kernel, height=height, width=width),
        out_shape=buf_shapes
        + (jax.ShapeDtypeStruct((layers + 1, total_steps, rows, chans), jnp.bfloat16),),
        grid_spec=pltpu.PrefetchScalarGridSpec(
            num_scalar_prefetch=1,
            grid=(1,),
            in_specs=fwd_in,
            out_specs=[slot_spec, slot_spec, slot_spec, pl.BlockSpec(memory_space=pl.ANY)],
        ),
        compiler_params=params,
        cost_estimate=fwd_cost,
    )(jnp.reshape(picked, (1,)).astype(jnp.int32), x_all, weights, kerns)

    carried = jnp.zeros((rows, chans), jnp.bfloat16)
    is_last = (my_section == sections - 1).astype(jnp.int32)
    for step in range(total_steps):
        picked, valid = picked_at(step)
        scalars = jnp.stack([picked, is_last, valid]).astype(jnp.int32)
        grid_spec = pltpu.PrefetchScalarGridSpec(
            num_scalar_prefetch=1,
            grid=(1,),
            in_specs=[
                pl.BlockSpec((None, rows, chans), lambda i, p: (p[0], 0, 0)),
                pl.BlockSpec((rows, chans), lambda i, p: (0, 0)),
                pl.BlockSpec((layers, None, rows, chans), lambda i, p: (0, p[0], 0, 0)),
                pl.BlockSpec((layers, chans, chans), lambda i, p: (0, 0, 0)),
                pl.BlockSpec((layers, taps, chans), lambda i, p: (0, 0, 0)),
                pl.BlockSpec(memory_space=pl.ANY),
            ],
            out_specs=[
                pl.BlockSpec((rows, chans), lambda i, p: (0, 0)),
                pl.BlockSpec(
                    (layers + 1, None, rows, chans), lambda i, p, s=step: (0, s, 0, 0)
                ),
            ],
        )
        g, hbuf = pl.pallas_call(
            functools.partial(step_kernel, height=height, width=width),
            out_shape=(
                jax.ShapeDtypeStruct((rows, chans), jnp.bfloat16),
                jax.ShapeDtypeStruct(hbuf.shape, jnp.bfloat16),
            ),
            grid_spec=grid_spec,
            input_output_aliases={6: 1},
            compiler_params=params,
            cost_estimate=fwd_cost,
        )(scalars, top_all, carried, zbuf, weights, kerns, hbuf)
        if step < total_steps - 1:
            carried = from_behind(g, "section", -1)
            nxt, _ = picked_at(step + 1)
            zbuf, abuf, xbuf = pl.pallas_call(
                functools.partial(fwd_kernel, height=height, width=width),
                out_shape=buf_shapes,
                grid_spec=pltpu.PrefetchScalarGridSpec(
                    num_scalar_prefetch=1,
                    grid=(1,),
                    in_specs=fwd_in + [pl.BlockSpec(memory_space=pl.ANY)] * 3,
                    out_specs=[slot_spec, slot_spec, slot_spec],
                ),
                input_output_aliases={4: 0, 5: 1, 6: 2},
                compiler_params=params,
                cost_estimate=fwd_cost,
            )(jnp.reshape(nxt, (1,)).astype(jnp.int32), x_all, weights, kerns, zbuf, abuf, xbuf)
    zs = zbuf.reshape(layers, batches * rows, chans)
    acts = abuf.reshape(layers, batches * rows, chans)
    xs = xbuf.reshape(layers, batches * rows, chans)

    count = batches * images * replicas * height * width
    scale = 1.0 / float(count) ** 0.5
    share = chans // replicas
    pad_taps = -(-taps // 16) * 16
    first = jnp.reshape(sections - 1 - my_section, (1,)).astype(jnp.int32)
    send, res = pl.pallas_call(
        functools.partial(grad_kernel, height=height, width=width, scale=scale),
        out_shape=(
            jax.ShapeDtypeStruct(lead + (layers * share + pad_taps, chans), jnp.bfloat16),
            jax.ShapeDtypeStruct((batches, rows, chans), jnp.bfloat16),
        ),
        in_specs=[smem, vmem, vmem, vmem, vmem, vmem, vmem],
        out_specs=(vmem, vmem),
        compiler_params=params,
    )(first, hbuf, acts, xs, zs, weights, kerns)
    part = send
    for axis, name in reversed(list(enumerate(("y", "z", "core")))):
        part = lax.all_to_all(part, name, axis, axis, tiled=True)
        part = jnp.sum(part.astype(jnp.float32), axis=axis)
        if axis:
            part = part.astype(jnp.bfloat16)
    summed = part
    point_red = summed[: layers * share].reshape(layers, share, chans)
    depth_red = summed[layers * share : layers * share + taps, : layers * share]
    depth_red = depth_red.reshape(taps, layers, share).transpose(1, 0, 2)
    results = res.reshape(inputs.shape)
    return (results[None], point_red[None], depth_red[None])


def solution(mesh):
    sections, replicas = mesh.devices.shape
    try:
        zsize = len({d.coords[2] for d in mesh.devices[0]})
    except (AttributeError, IndexError, TypeError):
        zsize = 1
    split = Mesh(
        mesh.devices.reshape(sections, replicas // (2 * zsize), zsize, 2),
        ("section", "y", "z", "core"),
    )
    dp = ("y", "z", "core")
    return jax.shard_map(
        body,
        mesh=split,
        in_specs=(
            P("section", None, dp, None, None, None),
            P(None, dp, None, None, None),
            P("section", None, None, None),
            P("section", None, None, None),
        ),
        out_specs=(
            P("section", None, dp, None, None, None),
            P("section", None, dp, None),
            P("section", None, None, dp),
        ),
        check_vma=False,
    )
```

```python
import functools
import math

import jax
import numpy as np
import jax.numpy as jnp
from jax import lax
from jax.experimental import pallas as pl
from jax.experimental.pallas import tpu as pltpu
from jax.sharding import Mesh, PartitionSpec as P

VMEM_LIMIT = 60 * 1024 * 1024


def from_behind(shard, axis, by):
    devices = lax.axis_size(axis)
    pairs = [(i, i + by) for i in range(devices) if 0 <= i + by < devices]
    return lax.ppermute(shard, axis, pairs)


def shift_rows(x, off):
    rows = x.shape[0]
    amount = (-off) % rows
    return x if amount == 0 else pltpu.roll(x, amount, 0)


def edge_masks(shape, height, width):
    r = lax.broadcasted_iota(jnp.int32, shape, 0)
    if width & (width - 1) == 0 and height & (height - 1) == 0:
        j = r & (width - 1)
        i = lax.shift_right_logical(r, width.bit_length() - 1) & (height - 1)
    else:
        j = lax.rem(r, width)
        i = lax.rem(lax.div(r, width), height)
    return {
        ("i", -1): i >= 1,
        ("i", 1): i < height - 1,
        ("j", -1): j >= 1,
        ("j", 1): j < width - 1,
    }


def offsets():
    for di in (-1, 0, 1):
        for dj in (-1, 0, 1):
            yield 3 * (di + 1) + (dj + 1), di, dj


def shifted_taps(x, masks, width, sign):
    cols = {}
    for dj in (-1, 0, 1):
        s = sign * dj
        cols[dj] = x if s == 0 else jnp.where(masks[("j", s)], shift_rows(x, s), 0.0)
    for tap, di, dj in offsets():
        s = sign * di
        c = cols[dj]
        yield tap, (c if s == 0 else jnp.where(masks[("i", s)], shift_rows(c, s * width), 0.0))


def stencil(x, k_ref, layer, masks, width, sign):
    total = jnp.zeros(x.shape, jnp.float32)
    for tap, moved in shifted_taps(x, masks, width, sign):
        total = total + k_ref[layer, tap : tap + 1, :] * moved
    return total


def fwd_kernel(p_ref, x_ref, w_ref, k_ref, *refs, height, width):
    z_ref, a_ref, xs_ref = refs[-3:]
    layers = w_ref.shape[0]
    field = x_ref[...]
    masks = edge_masks(field.shape, height, width)
    for layer in range(layers):
        xs_ref[layer] = field
        xf = field.astype(jnp.float32)
        zed = stencil(xf, k_ref, layer, masks, width, 1)
        z_ref[layer] = zed
        act = (zed * jax.nn.sigmoid(zed)).astype(jnp.bfloat16)
        a_ref[layer] = act
        branch = jnp.dot(act, w_ref[layer], preferred_element_type=jnp.float32)
        field = (xf + branch).astype(jnp.bfloat16)


def fwd_first_kernel(p_ref, x_ref, w_ref, k_ref, z_ref, a_ref, xs_ref, h_ref, *, height, width):
    del h_ref
    fwd_kernel(p_ref, x_ref, w_ref, k_ref, z_ref, a_ref, xs_ref, height=height, width=width)


def step_kernel(p_ref, top_ref, car_ref, z_ref, w_ref, k_ref, h_in, g_ref, h_ref, *, height, width):
    del h_in
    layers = w_ref.shape[0]
    top = top_ref[...].astype(jnp.float32)
    car = car_ref[...].astype(jnp.float32)
    g = jnp.where(p_ref[1] == 1, top, car)
    g = jnp.where(p_ref[2] == 1, g, 0.0).astype(jnp.bfloat16)
    h_ref[layers] = g
    masks = edge_masks(g.shape, height, width)
    for layer in reversed(range(layers)):
        back = lax.dot_general(
            g, w_ref[layer], (((1,), (1,)), ((), ())), preferred_element_type=jnp.float32
        )
        zed = z_ref[layer]
        sig = jax.nn.sigmoid(zed)
        dzed = back * sig * (1.0 + zed * (1.0 - sig))
        g = (g.astype(jnp.float32) + stencil(dzed, k_ref, layer, masks, width, -1)).astype(
            jnp.bfloat16
        )
        h_ref[layer] = g
    g_ref[...] = g


def grad_kernel(
    p_ref, h_ref, a_ref, xs_ref, z_ref, w_ref, k_ref, send_ref, res_ref, *, height, width, scale
):
    layers, chans = w_ref.shape[0], w_ref.shape[2]
    taps = k_ref.shape[1]
    batches = res_ref.shape[0]
    rows = h_ref.shape[2]
    lead = send_ref.shape[:-2]
    replicas = math.prod(lead)
    share = chans // replicas
    pad_taps = send_ref.shape[-2] - layers * share
    first = p_ref[0]
    for m in range(batches):
        res_ref[m] = h_ref[0, first + m]
    depth = []
    masks = edge_masks((batches * rows, chans), height, width)
    for layer in range(layers):
        g = h_ref[layer + 1, pl.ds(first, batches)].reshape(batches * rows, chans)
        back = lax.dot_general(
            g, w_ref[layer], (((1,), (1,)), ((), ())), preferred_element_type=jnp.float32
        )
        zed = z_ref[layer]
        sig = jax.nn.sigmoid(zed)
        dzed = back * sig * (1.0 + zed * (1.0 - sig))
        point = lax.dot_general(
            a_ref[layer], g, (((0,), (0,)), ((), ())), preferred_element_type=jnp.float32
        )
        point = point * scale
        for d in range(replicas):
            send_ref[np.unravel_index(d, lead) + (slice(layer * share, (layer + 1) * share),)] = point[
                d * share : (d + 1) * share
            ].astype(jnp.bfloat16)
        xf = xs_ref[layer].astype(jnp.float32)
        rows_out = []
        for tap, moved in shifted_taps(xf, masks, width, 1):
            rows_out.append(jnp.sum(moved * dzed, axis=0, keepdims=True))
        main = jnp.concatenate(rows_out[:pad_taps], axis=0) * scale
        extra = jnp.broadcast_to(rows_out[pad_taps] * scale, (pad_taps, chans))
        depth.append((main, extra))
    lane = lax.broadcasted_iota(jnp.int32, (pad_taps, chans), 1)
    row = lax.broadcasted_iota(jnp.int32, (pad_taps, chans), 0)
    for d in range(replicas):
        slot = jnp.zeros((pad_taps, chans), jnp.float32)
        for layer in range(layers):
            main, extra = depth[layer]
            amount = (layer * share - d * share) % chans
            moved = main if amount == 0 else pltpu.roll(main, amount, 1)
            keep = (lane >= layer * share) & (lane < (layer + 1) * share)
            slot = jnp.where(keep, moved, slot)
            start = layers * share + layer * share
            amount = (start - d * share) % chans
            moved = extra if amount == 0 else pltpu.roll(extra, amount, 1)
            keep = (row == 0) & (lane >= start) & (lane < start + share)
            slot = jnp.where(keep, moved, slot)
        send_ref[np.unravel_index(d, lead) + (slice(layers * share, None),)] = slot.astype(
            jnp.bfloat16
        )


def body(section_inputs, grad_out, point_weights, depth_weights):
    sections = lax.axis_size("section")
    lead = (lax.axis_size("chip"), lax.axis_size("core"))
    replicas = math.prod(lead)
    my_section = lax.axis_index("section")
    batches = grad_out.shape[0]
    layers = point_weights.shape[1]
    chans = point_weights.shape[3]
    taps = depth_weights.shape[2]
    inputs = section_inputs[0]
    images, height, width = inputs.shape[1], inputs.shape[2], inputs.shape[3]
    rows = images * height * width
    weights = point_weights[0]
    kerns = depth_weights[0].astype(jnp.float32)
    vmem = pl.BlockSpec(memory_space=pltpu.VMEM)
    smem = pl.BlockSpec(memory_space=pltpu.SMEM)
    params = pltpu.CompilerParams(vmem_limit_bytes=VMEM_LIMIT)

    fwd_flops = 2 * layers * rows * chans * (chans + 3 * taps)
    fwd_cost = pl.CostEstimate(
        flops=fwd_flops,
        transcendentals=layers * rows * chans,
        bytes_accessed=2 * layers * chans * chans + 8 * layers * rows * chans,
    )
    top_all = grad_out.reshape(batches, rows, chans)
    x_all = inputs.reshape(batches, rows, chans)
    total_steps = batches + sections - 1
    buf_shapes = (
        jax.ShapeDtypeStruct((layers, batches, rows, chans), jnp.float32),
        jax.ShapeDtypeStruct((layers, batches, rows, chans), jnp.bfloat16),
        jax.ShapeDtypeStruct((layers, batches, rows, chans), jnp.bfloat16),
    )
    slot_spec = pl.BlockSpec((layers, None, rows, chans), lambda i, p: (0, p[0], 0, 0))
    fwd_in = [
        pl.BlockSpec((None, rows, chans), lambda i, p: (p[0], 0, 0)),
        pl.BlockSpec((layers, chans, chans), lambda i, p: (0, 0, 0)),
        pl.BlockSpec((layers, taps, chans), lambda i, p: (0, 0, 0)),
    ]

    def picked_at(step):
        batch_id = step - (sections - 1) + my_section
        valid = ((batch_id >= 0) & (batch_id < batches)).astype(jnp.int32)
        return jnp.clip(batch_id, 0, batches - 1), valid

    picked, _ = picked_at(0)
    zbuf, abuf, xbuf, hbuf = pl.pallas_call(
        functools.partial(fwd_first_kernel, height=height, width=width),
        out_shape=buf_shapes
        + (jax.ShapeDtypeStruct((layers + 1, total_steps, rows, chans), jnp.bfloat16),),
        grid_spec=pltpu.PrefetchScalarGridSpec(
            num_scalar_prefetch=1,
            grid=(1,),
            in_specs=fwd_in,
            out_specs=[slot_spec, slot_spec, slot_spec, pl.BlockSpec(memory_space=pl.ANY)],
        ),
        compiler_params=params,
        cost_estimate=fwd_cost,
    )(jnp.reshape(picked, (1,)).astype(jnp.int32), x_all, weights, kerns)

    carried = jnp.zeros((rows, chans), jnp.bfloat16)
    is_last = (my_section == sections - 1).astype(jnp.int32)
    for step in range(total_steps):
        picked, valid = picked_at(step)
        scalars = jnp.stack([picked, is_last, valid]).astype(jnp.int32)
        grid_spec = pltpu.PrefetchScalarGridSpec(
            num_scalar_prefetch=1,
            grid=(1,),
            in_specs=[
                pl.BlockSpec((None, rows, chans), lambda i, p: (p[0], 0, 0)),
                pl.BlockSpec((rows, chans), lambda i, p: (0, 0)),
                pl.BlockSpec((layers, None, rows, chans), lambda i, p: (0, p[0], 0, 0)),
                pl.BlockSpec((layers, chans, chans), lambda i, p: (0, 0, 0)),
                pl.BlockSpec((layers, taps, chans), lambda i, p: (0, 0, 0)),
                pl.BlockSpec(memory_space=pl.ANY),
            ],
            out_specs=[
                pl.BlockSpec((rows, chans), lambda i, p: (0, 0)),
                pl.BlockSpec(
                    (layers + 1, None, rows, chans), lambda i, p, s=step: (0, s, 0, 0)
                ),
            ],
        )
        g, hbuf = pl.pallas_call(
            functools.partial(step_kernel, height=height, width=width),
            out_shape=(
                jax.ShapeDtypeStruct((rows, chans), jnp.bfloat16),
                jax.ShapeDtypeStruct(hbuf.shape, jnp.bfloat16),
            ),
            grid_spec=grid_spec,
            input_output_aliases={6: 1},
            compiler_params=params,
            cost_estimate=fwd_cost,
        )(scalars, top_all, carried, zbuf, weights, kerns, hbuf)
        if step < total_steps - 1:
            carried = from_behind(g, "section", -1)
            nxt, _ = picked_at(step + 1)
            zbuf, abuf, xbuf = pl.pallas_call(
                functools.partial(fwd_kernel, height=height, width=width),
                out_shape=buf_shapes,
                grid_spec=pltpu.PrefetchScalarGridSpec(
                    num_scalar_prefetch=1,
                    grid=(1,),
                    in_specs=fwd_in + [pl.BlockSpec(memory_space=pl.ANY)] * 3,
                    out_specs=[slot_spec, slot_spec, slot_spec],
                ),
                input_output_aliases={4: 0, 5: 1, 6: 2},
                compiler_params=params,
                cost_estimate=fwd_cost,
            )(jnp.reshape(nxt, (1,)).astype(jnp.int32), x_all, weights, kerns, zbuf, abuf, xbuf)
    zs = zbuf.reshape(layers, batches * rows, chans)
    acts = abuf.reshape(layers, batches * rows, chans)
    xs = xbuf.reshape(layers, batches * rows, chans)

    count = batches * images * replicas * height * width
    scale = 1.0 / float(count) ** 0.5
    share = chans // replicas
    pad_taps = taps - 1
    first = jnp.reshape(sections - 1 - my_section, (1,)).astype(jnp.int32)
    send, res = pl.pallas_call(
        functools.partial(grad_kernel, height=height, width=width, scale=scale),
        out_shape=(
            jax.ShapeDtypeStruct(lead + (layers * share + pad_taps, chans), jnp.bfloat16),
            jax.ShapeDtypeStruct((batches, rows, chans), jnp.bfloat16),
        ),
        in_specs=[smem, vmem, vmem, vmem, vmem, vmem, vmem],
        out_specs=(vmem, vmem),
        compiler_params=params,
    )(first, hbuf, acts, xs, zs, weights, kerns)
    part = send
    for axis, name in reversed(list(enumerate(("chip", "core")))):
        part = lax.all_to_all(part, name, axis, axis, tiled=True)
        part = jnp.sum(part.astype(jnp.float32), axis=axis)
        if axis:
            part = part.astype(jnp.bfloat16)
    summed = part
    point_red = summed[: layers * share].reshape(layers, share, chans)
    dk_rows = summed[layers * share : layers * share + pad_taps]
    depth_red = jnp.concatenate(
        [dk_rows[:, : layers * share], dk_rows[:1, layers * share : 2 * layers * share]], axis=0
    )
    depth_red = depth_red.reshape(taps, layers, share).transpose(1, 0, 2)
    results = res.reshape(inputs.shape)
    return (results[None], point_red[None], depth_red[None])


def solution(mesh):
    sections, replicas = mesh.devices.shape
    split = Mesh(mesh.devices.reshape(sections, replicas // 2, 2), ("section", "chip", "core"))
    dp = ("chip", "core")
    return jax.shard_map(
        body,
        mesh=split,
        in_specs=(
            P("section", None, dp, None, None, None),
            P(None, dp, None, None, None),
            P("section", None, None, None),
            P("section", None, None, None),
        ),
        out_specs=(
            P("section", None, dp, None, None, None),
            P("section", None, dp, None),
            P("section", None, None, dp),
        ),
        check_vma=False,
    )
```

```python
import functools
import math

import jax
import numpy as np
import jax.numpy as jnp
from jax import lax
from jax.experimental import pallas as pl
from jax.experimental.pallas import tpu as pltpu
from jax.sharding import Mesh, PartitionSpec as P

VMEM_LIMIT = 60 * 1024 * 1024


def from_behind(shard, axis, by):
    devices = lax.axis_size(axis)
    pairs = [(i, i + by) for i in range(devices) if 0 <= i + by < devices]
    return lax.ppermute(shard, axis, pairs)


def shift_rows(x, off):
    rows = x.shape[0]
    amount = (-off) % rows
    return x if amount == 0 else pltpu.roll(x, amount, 0)


def edge_masks(shape, height, width):
    r = lax.broadcasted_iota(jnp.int32, shape, 0)
    if width & (width - 1) == 0 and height & (height - 1) == 0:
        j = r & (width - 1)
        i = lax.shift_right_logical(r, width.bit_length() - 1) & (height - 1)
    else:
        j = lax.rem(r, width)
        i = lax.rem(lax.div(r, width), height)
    return {
        ("i", -1): i >= 1,
        ("i", 1): i < height - 1,
        ("j", -1): j >= 1,
        ("j", 1): j < width - 1,
    }


def offsets():
    for di in (-1, 0, 1):
        for dj in (-1, 0, 1):
            yield 3 * (di + 1) + (dj + 1), di, dj


def shifted_taps(x, masks, width, sign):
    cols = {}
    for dj in (-1, 0, 1):
        s = sign * dj
        cols[dj] = x if s == 0 else jnp.where(masks[("j", s)], shift_rows(x, s), 0.0)
    for tap, di, dj in offsets():
        s = sign * di
        c = cols[dj]
        yield tap, (c if s == 0 else jnp.where(masks[("i", s)], shift_rows(c, s * width), 0.0))


def stencil(x, k_ref, layer, masks, width, sign):
    total = jnp.zeros(x.shape, jnp.float32)
    for tap, moved in shifted_taps(x, masks, width, sign):
        total = total + k_ref[layer, tap : tap + 1, :] * moved
    return total


def fwd_kernel(p_ref, x_ref, w_ref, k_ref, *refs, height, width):
    z_ref, a_ref, xs_ref = refs[-3:]
    layers = w_ref.shape[0]
    field = x_ref[...]
    masks = edge_masks(field.shape, height, width)
    for layer in range(layers):
        xs_ref[layer] = field
        xf = field.astype(jnp.float32)
        zed = stencil(xf, k_ref, layer, masks, width, 1)
        z_ref[layer] = zed
        act = (zed * jax.nn.sigmoid(zed)).astype(jnp.bfloat16)
        a_ref[layer] = act
        branch = jnp.dot(act, w_ref[layer], preferred_element_type=jnp.float32)
        field = (xf + branch).astype(jnp.bfloat16)


def fwd_first_kernel(p_ref, x_ref, w_ref, k_ref, z_ref, a_ref, xs_ref, h_ref, *, height, width):
    del h_ref
    fwd_kernel(p_ref, x_ref, w_ref, k_ref, z_ref, a_ref, xs_ref, height=height, width=width)


def step_kernel(p_ref, top_ref, car_ref, z_ref, w_ref, k_ref, h_in, g_ref, h_ref, *, height, width):
    del h_in
    layers = w_ref.shape[0]
    top = top_ref[...].astype(jnp.float32)
    car = car_ref[...].astype(jnp.float32)
    g = jnp.where(p_ref[1] == 1, top, car)
    g = jnp.where(p_ref[2] == 1, g, 0.0).astype(jnp.bfloat16)
    h_ref[layers] = g
    masks = edge_masks(g.shape, height, width)
    for layer in reversed(range(layers)):
        back = lax.dot_general(
            g, w_ref[layer], (((1,), (1,)), ((), ())), preferred_element_type=jnp.float32
        )
        zed = z_ref[layer]
        sig = jax.nn.sigmoid(zed)
        dzed = back * sig * (1.0 + zed * (1.0 - sig))
        g = (g.astype(jnp.float32) + stencil(dzed, k_ref, layer, masks, width, -1)).astype(
            jnp.bfloat16
        )
        h_ref[layer] = g
    g_ref[...] = g


def grad_kernel(
    p_ref, h_ref, a_ref, xs_ref, z_ref, w_ref, k_ref, send_ref, res_ref, *, height, width, scale
):
    layers, chans = w_ref.shape[0], w_ref.shape[2]
    taps = k_ref.shape[1]
    batches = res_ref.shape[0]
    rows = h_ref.shape[2]
    lead = send_ref.shape[:-2]
    replicas = math.prod(lead)
    share = chans // replicas
    pad_taps = send_ref.shape[-2] - layers * share
    first = p_ref[0]
    for m in range(batches):
        res_ref[m] = h_ref[0, first + m]
    depth = []
    masks = edge_masks((batches * rows, chans), height, width)
    for layer in range(layers):
        g = h_ref[layer + 1, pl.ds(first, batches)].reshape(batches * rows, chans)
        back = lax.dot_general(
            g, w_ref[layer], (((1,), (1,)), ((), ())), preferred_element_type=jnp.float32
        )
        zed = z_ref[layer]
        sig = jax.nn.sigmoid(zed)
        dzed = back * sig * (1.0 + zed * (1.0 - sig))
        point = lax.dot_general(
            a_ref[layer], g, (((0,), (0,)), ((), ())), preferred_element_type=jnp.float32
        )
        point = point * scale
        for d in range(replicas):
            send_ref[(d % lead[0], d // lead[0], slice(layer * share, (layer + 1) * share))] = point[
                d * share : (d + 1) * share
            ].astype(jnp.bfloat16)
        xf = xs_ref[layer].astype(jnp.float32)
        rows_out = []
        for tap, moved in shifted_taps(xf, masks, width, 1):
            rows_out.append(jnp.sum(moved * dzed, axis=0, keepdims=True))
        main = jnp.concatenate(rows_out[:pad_taps], axis=0) * scale
        extra = jnp.broadcast_to(rows_out[pad_taps] * scale, (pad_taps, chans))
        depth.append((main, extra))
    lane = lax.broadcasted_iota(jnp.int32, (pad_taps, chans), 1)
    row = lax.broadcasted_iota(jnp.int32, (pad_taps, chans), 0)
    for d in range(replicas):
        slot = jnp.zeros((pad_taps, chans), jnp.float32)
        for layer in range(layers):
            main, extra = depth[layer]
            amount = (layer * share - d * share) % chans
            moved = main if amount == 0 else pltpu.roll(main, amount, 1)
            keep = (lane >= layer * share) & (lane < (layer + 1) * share)
            slot = jnp.where(keep, moved, slot)
            start = layers * share + layer * share
            amount = (start - d * share) % chans
            moved = extra if amount == 0 else pltpu.roll(extra, amount, 1)
            keep = (row == 0) & (lane >= start) & (lane < start + share)
            slot = jnp.where(keep, moved, slot)
        send_ref[(d % lead[0], d // lead[0], slice(layers * share, None))] = slot.astype(
            jnp.bfloat16
        )


def body(section_inputs, grad_out, point_weights, depth_weights):
    sections = lax.axis_size("section")
    lead = (lax.axis_size("core"), lax.axis_size("chip"))
    replicas = math.prod(lead)
    my_section = lax.axis_index("section")
    batches = grad_out.shape[0]
    layers = point_weights.shape[1]
    chans = point_weights.shape[3]
    taps = depth_weights.shape[2]
    inputs = section_inputs[0]
    images, height, width = inputs.shape[1], inputs.shape[2], inputs.shape[3]
    rows = images * height * width
    weights = point_weights[0]
    kerns = depth_weights[0].astype(jnp.float32)
    vmem = pl.BlockSpec(memory_space=pltpu.VMEM)
    smem = pl.BlockSpec(memory_space=pltpu.SMEM)
    params = pltpu.CompilerParams(vmem_limit_bytes=VMEM_LIMIT)

    fwd_flops = 2 * layers * rows * chans * (chans + 3 * taps)
    fwd_cost = pl.CostEstimate(
        flops=fwd_flops,
        transcendentals=layers * rows * chans,
        bytes_accessed=2 * layers * chans * chans + 8 * layers * rows * chans,
    )
    top_all = grad_out.reshape(batches, rows, chans)
    x_all = inputs.reshape(batches, rows, chans)
    total_steps = batches + sections - 1
    buf_shapes = (
        jax.ShapeDtypeStruct((layers, batches, rows, chans), jnp.float32),
        jax.ShapeDtypeStruct((layers, batches, rows, chans), jnp.bfloat16),
        jax.ShapeDtypeStruct((layers, batches, rows, chans), jnp.bfloat16),
    )
    slot_spec = pl.BlockSpec((layers, None, rows, chans), lambda i, p: (0, p[0], 0, 0))
    fwd_in = [
        pl.BlockSpec((None, rows, chans), lambda i, p: (p[0], 0, 0)),
        pl.BlockSpec((layers, chans, chans), lambda i, p: (0, 0, 0)),
        pl.BlockSpec((layers, taps, chans), lambda i, p: (0, 0, 0)),
    ]

    def picked_at(step):
        batch_id = step - (sections - 1) + my_section
        valid = ((batch_id >= 0) & (batch_id < batches)).astype(jnp.int32)
        return jnp.clip(batch_id, 0, batches - 1), valid

    picked, _ = picked_at(0)
    zbuf, abuf, xbuf, hbuf = pl.pallas_call(
        functools.partial(fwd_first_kernel, height=height, width=width),
        out_shape=buf_shapes
        + (jax.ShapeDtypeStruct((layers + 1, total_steps, rows, chans), jnp.bfloat16),),
        grid_spec=pltpu.PrefetchScalarGridSpec(
            num_scalar_prefetch=1,
            grid=(1,),
            in_specs=fwd_in,
            out_specs=[slot_spec, slot_spec, slot_spec, pl.BlockSpec(memory_space=pl.ANY)],
        ),
        compiler_params=params,
        cost_estimate=fwd_cost,
    )(jnp.reshape(picked, (1,)).astype(jnp.int32), x_all, weights, kerns)

    carried = jnp.zeros((rows, chans), jnp.bfloat16)
    is_last = (my_section == sections - 1).astype(jnp.int32)
    for step in range(total_steps):
        picked, valid = picked_at(step)
        scalars = jnp.stack([picked, is_last, valid]).astype(jnp.int32)
        grid_spec = pltpu.PrefetchScalarGridSpec(
            num_scalar_prefetch=1,
            grid=(1,),
            in_specs=[
                pl.BlockSpec((None, rows, chans), lambda i, p: (p[0], 0, 0)),
                pl.BlockSpec((rows, chans), lambda i, p: (0, 0)),
                pl.BlockSpec((layers, None, rows, chans), lambda i, p: (0, p[0], 0, 0)),
                pl.BlockSpec((layers, chans, chans), lambda i, p: (0, 0, 0)),
                pl.BlockSpec((layers, taps, chans), lambda i, p: (0, 0, 0)),
                pl.BlockSpec(memory_space=pl.ANY),
            ],
            out_specs=[
                pl.BlockSpec((rows, chans), lambda i, p: (0, 0)),
                pl.BlockSpec(
                    (layers + 1, None, rows, chans), lambda i, p, s=step: (0, s, 0, 0)
                ),
            ],
        )
        g, hbuf = pl.pallas_call(
            functools.partial(step_kernel, height=height, width=width),
            out_shape=(
                jax.ShapeDtypeStruct((rows, chans), jnp.bfloat16),
                jax.ShapeDtypeStruct(hbuf.shape, jnp.bfloat16),
            ),
            grid_spec=grid_spec,
            input_output_aliases={6: 1},
            compiler_params=params,
            cost_estimate=fwd_cost,
        )(scalars, top_all, carried, zbuf, weights, kerns, hbuf)
        if step < total_steps - 1:
            carried = from_behind(g, "section", -1)
            nxt, _ = picked_at(step + 1)
            zbuf, abuf, xbuf = pl.pallas_call(
                functools.partial(fwd_kernel, height=height, width=width),
                out_shape=buf_shapes,
                grid_spec=pltpu.PrefetchScalarGridSpec(
                    num_scalar_prefetch=1,
                    grid=(1,),
                    in_specs=fwd_in + [pl.BlockSpec(memory_space=pl.ANY)] * 3,
                    out_specs=[slot_spec, slot_spec, slot_spec],
                ),
                input_output_aliases={4: 0, 5: 1, 6: 2},
                compiler_params=params,
                cost_estimate=fwd_cost,
            )(jnp.reshape(nxt, (1,)).astype(jnp.int32), x_all, weights, kerns, zbuf, abuf, xbuf)
    zs = zbuf.reshape(layers, batches * rows, chans)
    acts = abuf.reshape(layers, batches * rows, chans)
    xs = xbuf.reshape(layers, batches * rows, chans)

    count = batches * images * replicas * height * width
    scale = 1.0 / float(count) ** 0.5
    share = chans // replicas
    pad_taps = taps - 1
    first = jnp.reshape(sections - 1 - my_section, (1,)).astype(jnp.int32)
    send, res = pl.pallas_call(
        functools.partial(grad_kernel, height=height, width=width, scale=scale),
        out_shape=(
            jax.ShapeDtypeStruct(lead + (layers * share + pad_taps, chans), jnp.bfloat16),
            jax.ShapeDtypeStruct((batches, rows, chans), jnp.bfloat16),
        ),
        in_specs=[smem, vmem, vmem, vmem, vmem, vmem, vmem],
        out_specs=(vmem, vmem),
        compiler_params=params,
    )(first, hbuf, acts, xs, zs, weights, kerns)
    part = send
    for stage, name in enumerate(("core", "chip")):
        part = lax.all_to_all(part, name, 0, 0, tiled=True)
        part = jnp.sum(part.astype(jnp.float32), axis=0)
        if stage == 0:
            part = part.astype(jnp.bfloat16)
    summed = part
    point_red = summed[: layers * share].reshape(layers, share, chans)
    dk_rows = summed[layers * share : layers * share + pad_taps]
    depth_red = jnp.concatenate(
        [dk_rows[:, : layers * share], dk_rows[:1, layers * share : 2 * layers * share]], axis=0
    )
    depth_red = depth_red.reshape(taps, layers, share).transpose(1, 0, 2)
    results = res.reshape(inputs.shape)
    return (results[None], point_red[None], depth_red[None])


def solution(mesh):
    sections, replicas = mesh.devices.shape
    split = Mesh(mesh.devices.reshape(sections, replicas // 2, 2), ("section", "chip", "core"))
    dp = ("chip", "core")
    return jax.shard_map(
        body,
        mesh=split,
        in_specs=(
            P("section", None, dp, None, None, None),
            P(None, dp, None, None, None),
            P("section", None, None, None),
            P("section", None, None, None),
        ),
        out_specs=(
            P("section", None, dp, None, None, None),
            P("section", None, dp, None),
            P("section", None, None, dp),
        ),
        check_vma=False,
    )
```

```python
import functools
import math

import jax
import numpy as np
import jax.numpy as jnp
from jax import lax
from jax.experimental import pallas as pl
from jax.experimental.pallas import tpu as pltpu
from jax.sharding import Mesh, PartitionSpec as P

VMEM_LIMIT = 60 * 1024 * 1024


def from_behind(shard, axis, by):
    devices = lax.axis_size(axis)
    pairs = [(i, i + by) for i in range(devices) if 0 <= i + by < devices]
    return lax.ppermute(shard, axis, pairs)


def shift_rows(x, off):
    rows = x.shape[0]
    amount = (-off) % rows
    return x if amount == 0 else pltpu.roll(x, amount, 0)


def edge_masks(shape, height, width):
    r = lax.broadcasted_iota(jnp.int32, shape, 0)
    if width & (width - 1) == 0 and height & (height - 1) == 0:
        j = r & (width - 1)
        i = lax.shift_right_logical(r, width.bit_length() - 1) & (height - 1)
    else:
        j = lax.rem(r, width)
        i = lax.rem(lax.div(r, width), height)
    return {
        ("i", -1): i >= 1,
        ("i", 1): i < height - 1,
        ("j", -1): j >= 1,
        ("j", 1): j < width - 1,
    }


def offsets():
    for di in (-1, 0, 1):
        for dj in (-1, 0, 1):
            yield 3 * (di + 1) + (dj + 1), di, dj


def shifted_taps(x, masks, width, sign):
    cols = {}
    for dj in (-1, 0, 1):
        s = sign * dj
        cols[dj] = x if s == 0 else jnp.where(masks[("j", s)], shift_rows(x, s), 0.0)
    for tap, di, dj in offsets():
        s = sign * di
        c = cols[dj]
        yield tap, (c if s == 0 else jnp.where(masks[("i", s)], shift_rows(c, s * width), 0.0))


def stencil(x, k_ref, layer, masks, width, sign):
    total = jnp.zeros(x.shape, jnp.float32)
    for tap, moved in shifted_taps(x, masks, width, sign):
        total = total + k_ref[layer, tap : tap + 1, :] * moved
    return total


def fwd_kernel(p_ref, x_ref, w_ref, k_ref, *refs, height, width):
    z_ref, a_ref, xs_ref = refs[-3:]
    layers = w_ref.shape[0]
    field = x_ref[...]
    masks = edge_masks(field.shape, height, width)
    for layer in range(layers):
        xs_ref[layer] = field
        xf = field.astype(jnp.float32)
        zed = stencil(xf, k_ref, layer, masks, width, 1)
        z_ref[layer] = zed
        act = (zed * jax.nn.sigmoid(zed)).astype(jnp.bfloat16)
        a_ref[layer] = act
        branch = jnp.dot(act, w_ref[layer], preferred_element_type=jnp.float32)
        field = (xf + branch).astype(jnp.bfloat16)


def fwd_first_kernel(p_ref, x_ref, w_ref, k_ref, z_ref, a_ref, xs_ref, h_ref, *, height, width):
    del h_ref
    fwd_kernel(p_ref, x_ref, w_ref, k_ref, z_ref, a_ref, xs_ref, height=height, width=width)


def step_kernel(p_ref, top_ref, car_ref, z_ref, wt_ref, k_ref, h_in, g_ref, h_ref, *, height, width):
    del h_in
    layers = wt_ref.shape[0]
    top = top_ref[...].astype(jnp.float32)
    car = car_ref[...].astype(jnp.float32)
    g = jnp.where(p_ref[1] == 1, top, car)
    g = jnp.where(p_ref[2] == 1, g, 0.0).astype(jnp.bfloat16)
    h_ref[layers] = g
    masks = edge_masks(g.shape, height, width)
    for layer in reversed(range(layers)):
        back = jnp.dot(g, wt_ref[layer], preferred_element_type=jnp.float32)
        zed = z_ref[layer]
        sig = jax.nn.sigmoid(zed)
        dzed = back * sig * (1.0 + zed * (1.0 - sig))
        g = (g.astype(jnp.float32) + stencil(dzed, k_ref, layer, masks, width, -1)).astype(
            jnp.bfloat16
        )
        h_ref[layer] = g
    g_ref[...] = g


def grad_kernel(
    p_ref, h_ref, a_ref, xs_ref, z_ref, wt_ref, k_ref, send_ref, res_ref, *, height, width, scale
):
    layers, chans = wt_ref.shape[0], wt_ref.shape[2]
    taps = k_ref.shape[1]
    batches = res_ref.shape[0]
    rows = h_ref.shape[2]
    lead = send_ref.shape[:-2]
    replicas = math.prod(lead)
    share = chans // replicas
    pad_taps = send_ref.shape[-2] - layers * share
    first = p_ref[0]
    for m in range(batches):
        res_ref[m] = h_ref[0, first + m]
    depth = []
    masks = edge_masks((batches * rows, chans), height, width)
    for layer in range(layers):
        g = h_ref[layer + 1, pl.ds(first, batches)].reshape(batches * rows, chans)
        back = jnp.dot(g, wt_ref[layer], preferred_element_type=jnp.float32)
        zed = z_ref[layer]
        sig = jax.nn.sigmoid(zed)
        dzed = back * sig * (1.0 + zed * (1.0 - sig))
        point = lax.dot_general(
            a_ref[layer], g, (((0,), (0,)), ((), ())), preferred_element_type=jnp.float32
        )
        point = point * scale
        for d in range(replicas):
            send_ref[(d % lead[0], d // lead[0], slice(layer * share, (layer + 1) * share))] = point[
                d * share : (d + 1) * share
            ].astype(jnp.bfloat16)
        xf = xs_ref[layer].astype(jnp.float32)
        rows_out = []
        for tap, moved in shifted_taps(xf, masks, width, 1):
            rows_out.append(jnp.sum(moved * dzed, axis=0, keepdims=True))
        main = jnp.concatenate(rows_out[:pad_taps], axis=0) * scale
        extra = jnp.broadcast_to(rows_out[pad_taps] * scale, (pad_taps, chans))
        depth.append((main, extra))
    lane = lax.broadcasted_iota(jnp.int32, (pad_taps, chans), 1)
    row = lax.broadcasted_iota(jnp.int32, (pad_taps, chans), 0)
    for d in range(replicas):
        slot = jnp.zeros((pad_taps, chans), jnp.float32)
        for layer in range(layers):
            main, extra = depth[layer]
            amount = (layer * share - d * share) % chans
            moved = main if amount == 0 else pltpu.roll(main, amount, 1)
            keep = (lane >= layer * share) & (lane < (layer + 1) * share)
            slot = jnp.where(keep, moved, slot)
            start = layers * share + layer * share
            amount = (start - d * share) % chans
            moved = extra if amount == 0 else pltpu.roll(extra, amount, 1)
            keep = (row == 0) & (lane >= start) & (lane < start + share)
            slot = jnp.where(keep, moved, slot)
        send_ref[(d % lead[0], d // lead[0], slice(layers * share, None))] = slot.astype(
            jnp.bfloat16
        )


def body(section_inputs, grad_out, point_weights, depth_weights):
    sections = lax.axis_size("section")
    lead = (lax.axis_size("core"), lax.axis_size("chip"))
    replicas = math.prod(lead)
    my_section = lax.axis_index("section")
    batches = grad_out.shape[0]
    layers = point_weights.shape[1]
    chans = point_weights.shape[3]
    taps = depth_weights.shape[2]
    inputs = section_inputs[0]
    images, height, width = inputs.shape[1], inputs.shape[2], inputs.shape[3]
    rows = images * height * width
    weights = point_weights[0]
    kerns = depth_weights[0].astype(jnp.float32)
    weights_t = jnp.swapaxes(weights, 1, 2)
    vmem = pl.BlockSpec(memory_space=pltpu.VMEM)
    smem = pl.BlockSpec(memory_space=pltpu.SMEM)
    params = pltpu.CompilerParams(vmem_limit_bytes=VMEM_LIMIT)

    fwd_flops = 2 * layers * rows * chans * (chans + 3 * taps)
    fwd_cost = pl.CostEstimate(
        flops=fwd_flops,
        transcendentals=layers * rows * chans,
        bytes_accessed=2 * layers * chans * chans + 8 * layers * rows * chans,
    )
    top_all = grad_out.reshape(batches, rows, chans)
    x_all = inputs.reshape(batches, rows, chans)
    total_steps = batches + sections - 1
    buf_shapes = (
        jax.ShapeDtypeStruct((layers, batches, rows, chans), jnp.float32),
        jax.ShapeDtypeStruct((layers, batches, rows, chans), jnp.bfloat16),
        jax.ShapeDtypeStruct((layers, batches, rows, chans), jnp.bfloat16),
    )
    slot_spec = pl.BlockSpec((layers, None, rows, chans), lambda i, p: (0, p[0], 0, 0))
    fwd_in = [
        pl.BlockSpec((None, rows, chans), lambda i, p: (p[0], 0, 0)),
        pl.BlockSpec((layers, chans, chans), lambda i, p: (0, 0, 0)),
        pl.BlockSpec((layers, taps, chans), lambda i, p: (0, 0, 0)),
    ]

    def picked_at(step):
        batch_id = step - (sections - 1) + my_section
        valid = ((batch_id >= 0) & (batch_id < batches)).astype(jnp.int32)
        return jnp.clip(batch_id, 0, batches - 1), valid

    picked, _ = picked_at(0)
    zbuf, abuf, xbuf, hbuf = pl.pallas_call(
        functools.partial(fwd_first_kernel, height=height, width=width),
        out_shape=buf_shapes
        + (jax.ShapeDtypeStruct((layers + 1, total_steps, rows, chans), jnp.bfloat16),),
        grid_spec=pltpu.PrefetchScalarGridSpec(
            num_scalar_prefetch=1,
            grid=(1,),
            in_specs=fwd_in,
            out_specs=[slot_spec, slot_spec, slot_spec, pl.BlockSpec(memory_space=pl.ANY)],
        ),
        compiler_params=params,
        cost_estimate=fwd_cost,
    )(jnp.reshape(picked, (1,)).astype(jnp.int32), x_all, weights, kerns)

    carried = jnp.zeros((rows, chans), jnp.bfloat16)
    is_last = (my_section == sections - 1).astype(jnp.int32)
    for step in range(total_steps):
        picked, valid = picked_at(step)
        scalars = jnp.stack([picked, is_last, valid]).astype(jnp.int32)
        grid_spec = pltpu.PrefetchScalarGridSpec(
            num_scalar_prefetch=1,
            grid=(1,),
            in_specs=[
                pl.BlockSpec((None, rows, chans), lambda i, p: (p[0], 0, 0)),
                pl.BlockSpec((rows, chans), lambda i, p: (0, 0)),
                pl.BlockSpec((layers, None, rows, chans), lambda i, p: (0, p[0], 0, 0)),
                pl.BlockSpec((layers, chans, chans), lambda i, p: (0, 0, 0)),
                pl.BlockSpec((layers, taps, chans), lambda i, p: (0, 0, 0)),
                pl.BlockSpec(memory_space=pl.ANY),
            ],
            out_specs=[
                pl.BlockSpec((rows, chans), lambda i, p: (0, 0)),
                pl.BlockSpec(
                    (layers + 1, None, rows, chans), lambda i, p, s=step: (0, s, 0, 0)
                ),
            ],
        )
        g, hbuf = pl.pallas_call(
            functools.partial(step_kernel, height=height, width=width),
            out_shape=(
                jax.ShapeDtypeStruct((rows, chans), jnp.bfloat16),
                jax.ShapeDtypeStruct(hbuf.shape, jnp.bfloat16),
            ),
            grid_spec=grid_spec,
            input_output_aliases={6: 1},
            compiler_params=params,
            cost_estimate=fwd_cost,
        )(scalars, top_all, carried, zbuf, weights_t, kerns, hbuf)
        if step < total_steps - 1:
            carried = from_behind(g, "section", -1)
            nxt, _ = picked_at(step + 1)
            zbuf, abuf, xbuf = pl.pallas_call(
                functools.partial(fwd_kernel, height=height, width=width),
                out_shape=buf_shapes,
                grid_spec=pltpu.PrefetchScalarGridSpec(
                    num_scalar_prefetch=1,
                    grid=(1,),
                    in_specs=fwd_in + [pl.BlockSpec(memory_space=pl.ANY)] * 3,
                    out_specs=[slot_spec, slot_spec, slot_spec],
                ),
                input_output_aliases={4: 0, 5: 1, 6: 2},
                compiler_params=params,
                cost_estimate=fwd_cost,
            )(jnp.reshape(nxt, (1,)).astype(jnp.int32), x_all, weights, kerns, zbuf, abuf, xbuf)
    zs = zbuf.reshape(layers, batches * rows, chans)
    acts = abuf.reshape(layers, batches * rows, chans)
    xs = xbuf.reshape(layers, batches * rows, chans)

    count = batches * images * replicas * height * width
    scale = 1.0 / float(count) ** 0.5
    share = chans // replicas
    pad_taps = taps - 1
    first = jnp.reshape(sections - 1 - my_section, (1,)).astype(jnp.int32)
    send, res = pl.pallas_call(
        functools.partial(grad_kernel, height=height, width=width, scale=scale),
        out_shape=(
            jax.ShapeDtypeStruct(lead + (layers * share + pad_taps, chans), jnp.bfloat16),
            jax.ShapeDtypeStruct((batches, rows, chans), jnp.bfloat16),
        ),
        in_specs=[smem, vmem, vmem, vmem, vmem, vmem, vmem],
        out_specs=(vmem, vmem),
        compiler_params=params,
    )(first, hbuf, acts, xs, zs, weights_t, kerns)
    part = send
    for stage, name in enumerate(("core", "chip")):
        part = lax.all_to_all(part, name, 0, 0, tiled=True)
        part = jnp.sum(part.astype(jnp.float32), axis=0)
        if stage == 0:
            part = part.astype(jnp.bfloat16)
    summed = part
    point_red = summed[: layers * share].reshape(layers, share, chans)
    dk_rows = summed[layers * share : layers * share + pad_taps]
    depth_red = jnp.concatenate(
        [dk_rows[:, : layers * share], dk_rows[:1, layers * share : 2 * layers * share]], axis=0
    )
    depth_red = depth_red.reshape(taps, layers, share).transpose(1, 0, 2)
    results = res.reshape(inputs.shape)
    return (results[None], point_red[None], depth_red[None])


def solution(mesh):
    sections, replicas = mesh.devices.shape
    split = Mesh(mesh.devices.reshape(sections, replicas // 2, 2), ("section", "chip", "core"))
    dp = ("chip", "core")
    return jax.shard_map(
        body,
        mesh=split,
        in_specs=(
            P("section", None, dp, None, None, None),
            P(None, dp, None, None, None),
            P("section", None, None, None),
            P("section", None, None, None),
        ),
        out_specs=(
            P("section", None, dp, None, None, None),
            P("section", None, dp, None),
            P("section", None, None, dp),
        ),
        check_vma=False,
    )
```

```python
import functools
import math

import jax
import numpy as np
import jax.numpy as jnp
from jax import lax
from jax.experimental import pallas as pl
from jax.experimental.pallas import tpu as pltpu
from jax.sharding import Mesh, PartitionSpec as P

VMEM_LIMIT = 60 * 1024 * 1024


def from_behind(shard, axis, by):
    devices = lax.axis_size(axis)
    pairs = [(i, i + by) for i in range(devices) if 0 <= i + by < devices]
    return lax.ppermute(shard, axis, pairs)


def shift_rows(x, off):
    rows = x.shape[0]
    amount = (-off) % rows
    return x if amount == 0 else pltpu.roll(x, amount, 0)


def edge_masks(shape, height, width):
    r = lax.broadcasted_iota(jnp.int32, shape, 0)
    if width & (width - 1) == 0 and height & (height - 1) == 0:
        j = r & (width - 1)
        i = lax.shift_right_logical(r, width.bit_length() - 1) & (height - 1)
    else:
        j = lax.rem(r, width)
        i = lax.rem(lax.div(r, width), height)
    return {
        ("i", -1): i >= 1,
        ("i", 1): i < height - 1,
        ("j", -1): j >= 1,
        ("j", 1): j < width - 1,
    }


def offsets():
    for di in (-1, 0, 1):
        for dj in (-1, 0, 1):
            yield 3 * (di + 1) + (dj + 1), di, dj


def shifted_taps(x, masks, width, sign):
    cols = {}
    for dj in (-1, 0, 1):
        s = sign * dj
        cols[dj] = x if s == 0 else jnp.where(masks[("j", s)], shift_rows(x, s), 0.0)
    for tap, di, dj in offsets():
        s = sign * di
        c = cols[dj]
        yield tap, (c if s == 0 else jnp.where(masks[("i", s)], shift_rows(c, s * width), 0.0))


def stencil(x, k_ref, layer, masks, width, sign):
    total = jnp.zeros(x.shape, jnp.float32)
    for tap, moved in shifted_taps(x, masks, width, sign):
        total = total + k_ref[layer, tap : tap + 1, :].astype(jnp.float32) * moved
    return total


def fwd_kernel(p_ref, x_ref, w_ref, k_ref, *refs, height, width):
    z_ref, a_ref, xs_ref = refs[-3:]
    layers = w_ref.shape[0]
    field = x_ref[...]
    masks = edge_masks(field.shape, height, width)
    for layer in range(layers):
        xs_ref[layer] = field
        xf = field.astype(jnp.float32)
        zed = stencil(xf, k_ref, layer, masks, width, 1)
        z_ref[layer] = zed
        act = (zed * jax.nn.sigmoid(zed)).astype(jnp.bfloat16)
        a_ref[layer] = act
        branch = jnp.dot(act, w_ref[layer], preferred_element_type=jnp.float32)
        field = (xf + branch).astype(jnp.bfloat16)


def fwd_first_kernel(p_ref, x_ref, w_ref, k_ref, z_ref, a_ref, xs_ref, h_ref, *, height, width):
    del h_ref
    fwd_kernel(p_ref, x_ref, w_ref, k_ref, z_ref, a_ref, xs_ref, height=height, width=width)


def step_kernel(p_ref, top_ref, car_ref, z_ref, w_ref, k_ref, h_in, g_ref, h_ref, *, height, width):
    del h_in
    layers = w_ref.shape[0]
    top = top_ref[...].astype(jnp.float32)
    car = car_ref[...].astype(jnp.float32)
    g = jnp.where(p_ref[1] == 1, top, car)
    g = jnp.where(p_ref[2] == 1, g, 0.0).astype(jnp.bfloat16)
    h_ref[layers] = g
    masks = edge_masks(g.shape, height, width)
    for layer in reversed(range(layers)):
        back = lax.dot_general(
            g, w_ref[layer], (((1,), (1,)), ((), ())), preferred_element_type=jnp.float32
        )
        zed = z_ref[layer]
        sig = jax.nn.sigmoid(zed)
        dzed = back * sig * (1.0 + zed * (1.0 - sig))
        g = (g.astype(jnp.float32) + stencil(dzed, k_ref, layer, masks, width, -1)).astype(
            jnp.bfloat16
        )
        h_ref[layer] = g
    g_ref[...] = g


def grad_kernel(
    p_ref, h_ref, a_ref, xs_ref, z_ref, w_ref, k_ref, send_ref, res_ref, *, height, width, scale
):
    layers, chans = w_ref.shape[0], w_ref.shape[2]
    taps = k_ref.shape[1]
    batches = res_ref.shape[0]
    rows = h_ref.shape[2]
    lead = send_ref.shape[:-2]
    replicas = math.prod(lead)
    share = chans // replicas
    pad_taps = send_ref.shape[-2] - layers * share
    first = p_ref[0]
    for m in range(batches):
        res_ref[m] = h_ref[0, first + m]
    depth = []
    masks = edge_masks((batches * rows, chans), height, width)
    for layer in range(layers):
        g = h_ref[layer + 1, pl.ds(first, batches)].reshape(batches * rows, chans)
        back = lax.dot_general(
            g, w_ref[layer], (((1,), (1,)), ((), ())), preferred_element_type=jnp.float32
        )
        zed = z_ref[layer]
        sig = jax.nn.sigmoid(zed)
        dzed = back * sig * (1.0 + zed * (1.0 - sig))
        point = lax.dot_general(
            a_ref[layer], g, (((0,), (0,)), ((), ())), preferred_element_type=jnp.float32
        )
        point = point * scale
        for d in range(replicas):
            send_ref[(d % lead[0], d // lead[0], slice(layer * share, (layer + 1) * share))] = point[
                d * share : (d + 1) * share
            ].astype(jnp.bfloat16)
        xf = xs_ref[layer].astype(jnp.float32)
        rows_out = []
        for tap, moved in shifted_taps(xf, masks, width, 1):
            rows_out.append(jnp.sum(moved * dzed, axis=0, keepdims=True))
        main = jnp.concatenate(rows_out[:pad_taps], axis=0) * scale
        extra = jnp.broadcast_to(rows_out[pad_taps] * scale, (pad_taps, chans))
        depth.append((main, extra))
    lane = lax.broadcasted_iota(jnp.int32, (pad_taps, chans), 1)
    row = lax.broadcasted_iota(jnp.int32, (pad_taps, chans), 0)
    for d in range(replicas):
        slot = jnp.zeros((pad_taps, chans), jnp.float32)
        for layer in range(layers):
            main, extra = depth[layer]
            amount = (layer * share - d * share) % chans
            moved = main if amount == 0 else pltpu.roll(main, amount, 1)
            keep = (lane >= layer * share) & (lane < (layer + 1) * share)
            slot = jnp.where(keep, moved, slot)
            start = layers * share + layer * share
            amount = (start - d * share) % chans
            moved = extra if amount == 0 else pltpu.roll(extra, amount, 1)
            keep = (row == 0) & (lane >= start) & (lane < start + share)
            slot = jnp.where(keep, moved, slot)
        send_ref[(d % lead[0], d // lead[0], slice(layers * share, None))] = slot.astype(
            jnp.bfloat16
        )


def body(section_inputs, grad_out, point_weights, depth_weights):
    sections = lax.axis_size("section")
    lead = (lax.axis_size("core"), lax.axis_size("chip"))
    replicas = math.prod(lead)
    my_section = lax.axis_index("section")
    batches = grad_out.shape[0]
    layers = point_weights.shape[1]
    chans = point_weights.shape[3]
    taps = depth_weights.shape[2]
    inputs = section_inputs[0]
    images, height, width = inputs.shape[1], inputs.shape[2], inputs.shape[3]
    rows = images * height * width
    weights = point_weights[0]
    kerns = depth_weights[0]
    vmem = pl.BlockSpec(memory_space=pltpu.VMEM)
    smem = pl.BlockSpec(memory_space=pltpu.SMEM)
    params = pltpu.CompilerParams(vmem_limit_bytes=VMEM_LIMIT)

    fwd_flops = 2 * layers * rows * chans * (chans + 3 * taps)
    fwd_cost = pl.CostEstimate(
        flops=fwd_flops,
        transcendentals=layers * rows * chans,
        bytes_accessed=2 * layers * chans * chans + 8 * layers * rows * chans,
    )
    top_all = grad_out.reshape(batches, rows, chans)
    x_all = inputs.reshape(batches, rows, chans)
    total_steps = batches + sections - 1
    buf_shapes = (
        jax.ShapeDtypeStruct((layers, batches, rows, chans), jnp.float32),
        jax.ShapeDtypeStruct((layers, batches, rows, chans), jnp.bfloat16),
        jax.ShapeDtypeStruct((layers, batches, rows, chans), jnp.bfloat16),
    )
    slot_spec = pl.BlockSpec((layers, None, rows, chans), lambda i, p: (0, p[0], 0, 0))
    fwd_in = [
        pl.BlockSpec((None, rows, chans), lambda i, p: (p[0], 0, 0)),
        pl.BlockSpec((layers, chans, chans), lambda i, p: (0, 0, 0)),
        pl.BlockSpec((layers, taps, chans), lambda i, p: (0, 0, 0)),
    ]

    def picked_at(step):
        batch_id = step - (sections - 1) + my_section
        valid = ((batch_id >= 0) & (batch_id < batches)).astype(jnp.int32)
        return jnp.clip(batch_id, 0, batches - 1), valid

    picked, _ = picked_at(0)
    zbuf, abuf, xbuf, hbuf = pl.pallas_call(
        functools.partial(fwd_first_kernel, height=height, width=width),
        out_shape=buf_shapes
        + (jax.ShapeDtypeStruct((layers + 1, total_steps, rows, chans), jnp.bfloat16),),
        grid_spec=pltpu.PrefetchScalarGridSpec(
            num_scalar_prefetch=1,
            grid=(1,),
            in_specs=fwd_in,
            out_specs=[slot_spec, slot_spec, slot_spec, pl.BlockSpec(memory_space=pl.ANY)],
        ),
        compiler_params=params,
        cost_estimate=fwd_cost,
    )(jnp.reshape(picked, (1,)).astype(jnp.int32), x_all, weights, kerns)

    carried = top_all
    is_last = (my_section == sections - 1).astype(jnp.int32)
    for step in range(total_steps):
        picked, valid = picked_at(step)
        scalars = jnp.stack([picked, is_last, valid]).astype(jnp.int32)
        grid_spec = pltpu.PrefetchScalarGridSpec(
            num_scalar_prefetch=1,
            grid=(1,),
            in_specs=[
                pl.BlockSpec((None, rows, chans), lambda i, p: (p[0], 0, 0)),
                pl.BlockSpec((rows, chans), lambda i, p: (0, 0))
                if step
                else pl.BlockSpec((None, rows, chans), lambda i, p: (p[0], 0, 0)),
                pl.BlockSpec((layers, None, rows, chans), lambda i, p: (0, p[0], 0, 0)),
                pl.BlockSpec((layers, chans, chans), lambda i, p: (0, 0, 0)),
                pl.BlockSpec((layers, taps, chans), lambda i, p: (0, 0, 0)),
                pl.BlockSpec(memory_space=pl.ANY),
            ],
            out_specs=[
                pl.BlockSpec((rows, chans), lambda i, p: (0, 0)),
                pl.BlockSpec(
                    (layers + 1, None, rows, chans), lambda i, p, s=step: (0, s, 0, 0)
                ),
            ],
        )
        g, hbuf = pl.pallas_call(
            functools.partial(step_kernel, height=height, width=width),
            out_shape=(
                jax.ShapeDtypeStruct((rows, chans), jnp.bfloat16),
                jax.ShapeDtypeStruct(hbuf.shape, jnp.bfloat16),
            ),
            grid_spec=grid_spec,
            input_output_aliases={6: 1},
            compiler_params=params,
            cost_estimate=fwd_cost,
        )(scalars, top_all, carried, zbuf, weights, kerns, hbuf)
        if step < total_steps - 1:
            carried = from_behind(g, "section", -1)
            nxt, _ = picked_at(step + 1)
            zbuf, abuf, xbuf = pl.pallas_call(
                functools.partial(fwd_kernel, height=height, width=width),
                out_shape=buf_shapes,
                grid_spec=pltpu.PrefetchScalarGridSpec(
                    num_scalar_prefetch=1,
                    grid=(1,),
                    in_specs=fwd_in + [pl.BlockSpec(memory_space=pl.ANY)] * 3,
                    out_specs=[slot_spec, slot_spec, slot_spec],
                ),
                input_output_aliases={4: 0, 5: 1, 6: 2},
                compiler_params=params,
                cost_estimate=fwd_cost,
            )(jnp.reshape(nxt, (1,)).astype(jnp.int32), x_all, weights, kerns, zbuf, abuf, xbuf)
    zs = zbuf.reshape(layers, batches * rows, chans)
    acts = abuf.reshape(layers, batches * rows, chans)
    xs = xbuf.reshape(layers, batches * rows, chans)

    count = batches * images * replicas * height * width
    scale = 1.0 / float(count) ** 0.5
    share = chans // replicas
    pad_taps = taps - 1
    first = jnp.reshape(sections - 1 - my_section, (1,)).astype(jnp.int32)
    send, res = pl.pallas_call(
        functools.partial(grad_kernel, height=height, width=width, scale=scale),
        out_shape=(
            jax.ShapeDtypeStruct(lead + (layers * share + pad_taps, chans), jnp.bfloat16),
            jax.ShapeDtypeStruct((batches, rows, chans), jnp.bfloat16),
        ),
        in_specs=[smem, vmem, vmem, vmem, vmem, vmem, vmem],
        out_specs=(vmem, vmem),
        compiler_params=params,
    )(first, hbuf, acts, xs, zs, weights, kerns)
    part = send
    for stage, name in enumerate(("core", "chip")):
        part = lax.all_to_all(part, name, 0, 0, tiled=True)
        part = jnp.sum(part.astype(jnp.float32), axis=0)
        if stage == 0:
            part = part.astype(jnp.bfloat16)
    summed = part
    point_red = summed[: layers * share].reshape(layers, share, chans)
    dk_rows = summed[layers * share : layers * share + pad_taps]
    depth_red = jnp.concatenate(
        [dk_rows[:, : layers * share], dk_rows[:1, layers * share : 2 * layers * share]], axis=0
    )
    depth_red = depth_red.reshape(taps, layers, share).transpose(1, 0, 2)
    results = res.reshape(inputs.shape)
    return (results[None], point_red[None], depth_red[None])


def solution(mesh):
    sections, replicas = mesh.devices.shape
    split = Mesh(mesh.devices.reshape(sections, replicas // 2, 2), ("section", "chip", "core"))
    dp = ("chip", "core")
    return jax.shard_map(
        body,
        mesh=split,
        in_specs=(
            P("section", None, dp, None, None, None),
            P(None, dp, None, None, None),
            P("section", None, None, None),
            P("section", None, None, None),
        ),
        out_specs=(
            P("section", None, dp, None, None, None),
            P("section", None, dp, None),
            P("section", None, None, dp),
        ),
        check_vma=False,
    )
```

```python
import functools
import math

import jax
import numpy as np
import jax.numpy as jnp
from jax import lax
from jax.experimental import pallas as pl
from jax.experimental.pallas import tpu as pltpu
from jax.sharding import Mesh, PartitionSpec as P

VMEM_LIMIT = 60 * 1024 * 1024


def from_behind(shard, axis, by):
    devices = lax.axis_size(axis)
    pairs = [(i, i + by) for i in range(devices) if 0 <= i + by < devices]
    return lax.ppermute(shard, axis, pairs)


def shift_rows(x, off):
    rows = x.shape[0]
    amount = (-off) % rows
    return x if amount == 0 else pltpu.roll(x, amount, 0)


def edge_masks(shape, height, width):
    r = lax.broadcasted_iota(jnp.int32, shape, 0)
    if width & (width - 1) == 0 and height & (height - 1) == 0:
        j = r & (width - 1)
        i = lax.shift_right_logical(r, width.bit_length() - 1) & (height - 1)
    else:
        j = lax.rem(r, width)
        i = lax.rem(lax.div(r, width), height)
    return {
        ("i", -1): i >= 1,
        ("i", 1): i < height - 1,
        ("j", -1): j >= 1,
        ("j", 1): j < width - 1,
    }


def offsets():
    for di in (-1, 0, 1):
        for dj in (-1, 0, 1):
            yield 3 * (di + 1) + (dj + 1), di, dj


def shifted_taps(x, masks, width, sign):
    cols = {}
    for dj in (-1, 0, 1):
        s = sign * dj
        cols[dj] = x if s == 0 else jnp.where(masks[("j", s)], shift_rows(x, s), 0.0)
    for tap, di, dj in offsets():
        s = sign * di
        c = cols[dj]
        yield tap, (c if s == 0 else jnp.where(masks[("i", s)], shift_rows(c, s * width), 0.0))


def stencil(x, k_ref, layer, masks, width, sign):
    total = jnp.zeros(x.shape, jnp.float32)
    for tap, moved in shifted_taps(x, masks, width, sign):
        total = total + k_ref[layer, tap : tap + 1, :] * moved
    return total


def fwd_kernel(p_ref, x_ref, w_ref, k_ref, *refs, height, width):
    z_ref, a_ref, xs_ref = refs[-3:]
    layers = w_ref.shape[0]
    field = x_ref[...]
    masks = edge_masks(field.shape, height, width)
    for layer in range(layers):
        xs_ref[layer] = field
        xf = field.astype(jnp.float32)
        zed = stencil(xf, k_ref, layer, masks, width, 1)
        z_ref[layer] = zed
        act = (zed * jax.nn.sigmoid(zed)).astype(jnp.bfloat16)
        a_ref[layer] = act
        branch = jnp.dot(act, w_ref[layer], preferred_element_type=jnp.float32)
        field = (xf + branch).astype(jnp.bfloat16)


def fwd_first_kernel(p_ref, x_ref, w_ref, k_ref, z_ref, a_ref, xs_ref, h_ref, *, height, width):
    del h_ref
    fwd_kernel(p_ref, x_ref, w_ref, k_ref, z_ref, a_ref, xs_ref, height=height, width=width)


def step_kernel(p_ref, top_ref, car_ref, z_ref, w_ref, k_ref, h_in, g_ref, h_ref, *, height, width):
    del h_in
    layers = w_ref.shape[0]
    top = top_ref[...].astype(jnp.float32)
    car = car_ref[...].astype(jnp.float32)
    g = jnp.where(p_ref[1] == 1, top, car)
    g = jnp.where(p_ref[2] == 1, g, 0.0).astype(jnp.bfloat16)
    h_ref[layers] = g
    masks = edge_masks(g.shape, height, width)
    for layer in reversed(range(layers)):
        back = lax.dot_general(
            g, w_ref[layer], (((1,), (1,)), ((), ())), preferred_element_type=jnp.float32
        )
        zed = z_ref[layer]
        sig = jax.nn.sigmoid(zed)
        dzed = back * sig * (1.0 + zed * (1.0 - sig))
        g = (g.astype(jnp.float32) + stencil(dzed, k_ref, layer, masks, width, -1)).astype(
            jnp.bfloat16
        )
        h_ref[layer] = g
    g_ref[...] = g


def grad_kernel(
    p_ref, h_ref, a_ref, xs_ref, z_ref, w_ref, k_ref, send_ref, res_ref, *, height, width, scale
):
    layers, chans = w_ref.shape[0], w_ref.shape[2]
    taps = k_ref.shape[1]
    batches = res_ref.shape[0]
    rows = h_ref.shape[2]
    lead = send_ref.shape[:-2]
    replicas = math.prod(lead)
    share = chans // replicas
    pad_taps = send_ref.shape[-2] - layers * share
    first = p_ref[0]
    for m in range(batches):
        res_ref[m] = h_ref[0, first + m]
    depth = []
    masks = edge_masks((batches * rows, chans), height, width)
    for layer in range(layers):
        g = h_ref[layer + 1, pl.ds(first, batches)].reshape(batches * rows, chans)
        back = lax.dot_general(
            g, w_ref[layer], (((1,), (1,)), ((), ())), preferred_element_type=jnp.float32
        )
        zed = z_ref[layer]
        sig = jax.nn.sigmoid(zed)
        dzed = back * sig * (1.0 + zed * (1.0 - sig))
        point = lax.dot_general(
            a_ref[layer], g, (((0,), (0,)), ((), ())), preferred_element_type=jnp.float32
        )
        point = point * scale
        for d in range(replicas):
            send_ref[(d % lead[0], d // lead[0], slice(layer * share, (layer + 1) * share))] = point[
                d * share : (d + 1) * share
            ].astype(jnp.bfloat16)
        xf = xs_ref[layer].astype(jnp.float32)
        rows_out = []
        for tap, moved in shifted_taps(xf, masks, width, 1):
            rows_out.append(jnp.sum(moved * dzed, axis=0, keepdims=True))
        main = jnp.concatenate(rows_out[:pad_taps], axis=0) * scale
        extra = jnp.broadcast_to(rows_out[pad_taps] * scale, (pad_taps, chans))
        depth.append((main, extra))
    lane = lax.broadcasted_iota(jnp.int32, (pad_taps, chans), 1)
    row = lax.broadcasted_iota(jnp.int32, (pad_taps, chans), 0)
    for d in range(replicas):
        slot = jnp.zeros((pad_taps, chans), jnp.float32)
        for layer in range(layers):
            main, extra = depth[layer]
            amount = (layer * share - d * share) % chans
            moved = main if amount == 0 else pltpu.roll(main, amount, 1)
            keep = (lane >= layer * share) & (lane < (layer + 1) * share)
            slot = jnp.where(keep, moved, slot)
            start = layers * share + layer * share
            amount = (start - d * share) % chans
            moved = extra if amount == 0 else pltpu.roll(extra, amount, 1)
            keep = (row == 0) & (lane >= start) & (lane < start + share)
            slot = jnp.where(keep, moved, slot)
        send_ref[(d % lead[0], d // lead[0], slice(layers * share, None))] = slot.astype(
            jnp.bfloat16
        )


def body(section_inputs, grad_out, point_weights, depth_weights):
    sections = lax.axis_size("section")
    lead = (lax.axis_size("core"), lax.axis_size("chip"))
    replicas = math.prod(lead)
    my_section = lax.axis_index("section")
    batches = grad_out.shape[0]
    layers = point_weights.shape[1]
    chans = point_weights.shape[3]
    taps = depth_weights.shape[2]
    inputs = section_inputs[0]
    images, height, width = inputs.shape[1], inputs.shape[2], inputs.shape[3]
    rows = images * height * width
    weights = point_weights[0]
    kerns = depth_weights[0].astype(jnp.float32)
    vmem = pl.BlockSpec(memory_space=pltpu.VMEM)
    smem = pl.BlockSpec(memory_space=pltpu.SMEM)
    params = pltpu.CompilerParams(vmem_limit_bytes=VMEM_LIMIT)

    fwd_flops = 2 * layers * rows * chans * (chans + 3 * taps)
    fwd_cost = pl.CostEstimate(
        flops=fwd_flops,
        transcendentals=layers * rows * chans,
        bytes_accessed=2 * layers * chans * chans + 8 * layers * rows * chans,
    )
    top_all = grad_out.reshape(batches, rows, chans)
    x_all = inputs.reshape(batches, rows, chans)
    total_steps = batches + sections - 1
    buf_shapes = (
        jax.ShapeDtypeStruct((layers, batches, rows, chans), jnp.float32),
        jax.ShapeDtypeStruct((layers, batches, rows, chans), jnp.bfloat16),
        jax.ShapeDtypeStruct((layers, batches, rows, chans), jnp.bfloat16),
    )
    slot_spec = pl.BlockSpec((layers, None, rows, chans), lambda i, p: (0, p[0], 0, 0))
    fwd_in = [
        pl.BlockSpec((None, rows, chans), lambda i, p: (p[0], 0, 0)),
        pl.BlockSpec((layers, chans, chans), lambda i, p: (0, 0, 0)),
        pl.BlockSpec((layers, taps, chans), lambda i, p: (0, 0, 0)),
    ]

    def picked_at(step):
        batch_id = step - (sections - 1) + my_section
        valid = ((batch_id >= 0) & (batch_id < batches)).astype(jnp.int32)
        return jnp.clip(batch_id, 0, batches - 1), valid

    picked, _ = picked_at(0)
    zbuf, abuf, xbuf, hbuf = pl.pallas_call(
        functools.partial(fwd_first_kernel, height=height, width=width),
        out_shape=buf_shapes
        + (jax.ShapeDtypeStruct((layers + 1, total_steps, rows, chans), jnp.bfloat16),),
        grid_spec=pltpu.PrefetchScalarGridSpec(
            num_scalar_prefetch=1,
            grid=(1,),
            in_specs=fwd_in,
            out_specs=[slot_spec, slot_spec, slot_spec, pl.BlockSpec(memory_space=pl.ANY)],
        ),
        compiler_params=params,
        cost_estimate=fwd_cost,
    )(jnp.reshape(picked, (1,)).astype(jnp.int32), x_all, weights, kerns)

    carried = jnp.zeros((rows, chans), jnp.bfloat16)
    is_last = (my_section == sections - 1).astype(jnp.int32)
    for step in range(total_steps):
        picked, valid = picked_at(step)
        scalars = jnp.stack([picked, is_last, valid]).astype(jnp.int32)
        grid_spec = pltpu.PrefetchScalarGridSpec(
            num_scalar_prefetch=1,
            grid=(1,),
            in_specs=[
                pl.BlockSpec((None, rows, chans), lambda i, p: (p[0], 0, 0)),
                pl.BlockSpec((rows, chans), lambda i, p: (0, 0)),
                pl.BlockSpec((layers, None, rows, chans), lambda i, p: (0, p[0], 0, 0)),
                pl.BlockSpec((layers, chans, chans), lambda i, p: (0, 0, 0)),
                pl.BlockSpec((layers, taps, chans), lambda i, p: (0, 0, 0)),
                pl.BlockSpec(memory_space=pl.ANY),
            ],
            out_specs=[
                pl.BlockSpec((rows, chans), lambda i, p: (0, 0)),
                pl.BlockSpec(
                    (layers + 1, None, rows, chans), lambda i, p, s=step: (0, s, 0, 0)
                ),
            ],
        )
        g, hbuf = pl.pallas_call(
            functools.partial(step_kernel, height=height, width=width),
            out_shape=(
                jax.ShapeDtypeStruct((rows, chans), jnp.bfloat16),
                jax.ShapeDtypeStruct(hbuf.shape, jnp.bfloat16),
            ),
            grid_spec=grid_spec,
            input_output_aliases={6: 1},
            compiler_params=params,
            cost_estimate=fwd_cost,
        )(scalars, top_all, carried, zbuf, weights, kerns, hbuf)
        if step < total_steps - 1:
            carried = from_behind(g, "section", -1)
            nxt, _ = picked_at(step + 1)
            zbuf, abuf, xbuf = pl.pallas_call(
                functools.partial(fwd_kernel, height=height, width=width),
                out_shape=buf_shapes,
                grid_spec=pltpu.PrefetchScalarGridSpec(
                    num_scalar_prefetch=1,
                    grid=(1,),
                    in_specs=fwd_in + [pl.BlockSpec(memory_space=pl.ANY)] * 3,
                    out_specs=[slot_spec, slot_spec, slot_spec],
                ),
                input_output_aliases={4: 0, 5: 1, 6: 2},
                compiler_params=params,
                cost_estimate=fwd_cost,
            )(jnp.reshape(nxt, (1,)).astype(jnp.int32), x_all, weights, kerns, zbuf, abuf, xbuf)
    zs = zbuf.reshape(layers, batches * rows, chans)
    acts = abuf.reshape(layers, batches * rows, chans)
    xs = xbuf.reshape(layers, batches * rows, chans)

    count = batches * images * replicas * height * width
    scale = 1.0 / float(count) ** 0.5
    share = chans // replicas
    pad_taps = taps - 1
    first = jnp.reshape(sections - 1 - my_section, (1,)).astype(jnp.int32)
    send, res = pl.pallas_call(
        functools.partial(grad_kernel, height=height, width=width, scale=scale),
        out_shape=(
            jax.ShapeDtypeStruct(lead + (layers * share + pad_taps, chans), jnp.bfloat16),
            jax.ShapeDtypeStruct((batches, rows, chans), jnp.bfloat16),
        ),
        in_specs=[smem, vmem, vmem, vmem, vmem, vmem, vmem],
        out_specs=(vmem, vmem),
        compiler_params=params,
    )(first, hbuf, acts, xs, zs, weights, kerns)
    part = lax.all_to_all(send, "core", 0, 0, tiled=True)
    part = jnp.sum(part.astype(jnp.float32), axis=0).astype(jnp.bfloat16)
    recv = lax.all_to_all(part, "chip", 0, 0, tiled=True).astype(jnp.float32)
    point_red = jnp.sum(recv[:, : layers * share], axis=0).reshape(layers, share, chans)
    dk_rows = jnp.sum(recv[:, layers * share : layers * share + pad_taps], axis=0)
    depth_red = jnp.concatenate(
        [dk_rows[:, : layers * share], dk_rows[:1, layers * share : 2 * layers * share]], axis=0
    )
    depth_red = depth_red.reshape(taps, layers, share).transpose(1, 0, 2)
    results = res.reshape(inputs.shape)
    return (results[None], point_red[None], depth_red[None])


def solution(mesh):
    sections, replicas = mesh.devices.shape
    split = Mesh(mesh.devices.reshape(sections, replicas // 2, 2), ("section", "chip", "core"))
    dp = ("chip", "core")
    return jax.shard_map(
        body,
        mesh=split,
        in_specs=(
            P("section", None, dp, None, None, None),
            P(None, dp, None, None, None),
            P("section", None, None, None),
            P("section", None, None, None),
        ),
        out_specs=(
            P("section", None, dp, None, None, None),
            P("section", None, dp, None),
            P("section", None, None, dp),
        ),
        check_vma=False,
    )
```
